128 devices in a mesh: req: 16 (over z, y), tensor: 8 (over x, core).
Axes of the slice: x: 4, y: 4, z: 4, core: 2. Of those that a mesh axis runs over, the one named last changes fastest.
Arguments:
- residual_input: bfloat16 [8192, 7168], P('req', 'tensor'), may hold values from -6 to 6
- input_norm_gain: float32 [7168], replicated, may hold values from 0.25 to 1.75
- query_weight: bfloat16 [7168, 4096], P(None, 'tensor'), may hold values from -0.09375 to 0.09375
- key_value_weight: bfloat16 [7168, 2048], P(None, 'tensor'), may hold values from -0.09375 to 0.09375
- output_weight: bfloat16 [4096, 7168], P('tensor'), may hold values from -0.375 to 0.375
- adapter_down_maps: bfloat16 [64, 48, 7168], P('req', None, 'tensor'), may hold values from -0.0625 to 0.0625
- adapter_query_up: bfloat16 [64, 16, 4096], P('req', None, 'tensor'), may hold values from -0.375 to 0.375
- adapter_key_value_up: bfloat16 [64, 2, 16, 1024], P('req', None, None, 'tensor'), may hold values from -0.375 to 0.375
- adapter_output_down: bfloat16 [64, 16, 4096], P('req', None, 'tensor'), may hold values from -0.375 to 0.375
- adapter_output_up: bfloat16 [64, 16, 7168], P('req', None, 'tensor'), may hold values from -0.375 to 0.375
- request_adapter: int32 [64], P('req'), may hold values from 0 to 63
- prompt_length: int32 [64], P('req'), may hold values from 32 to 128, as said below
- cache_length: int32 [32], replicated, may hold values from 16 to 2048, as said below
- first_page_device: int32 [32], replicated, may hold values from 0 to 15
- page_slot_table: int32 [16, 32], P('req'), may hold values from 0 to 31, as said below
- cache_page_pool: bfloat16 [512, 128, 2048], P('req', None, 'tensor'), may hold values from -200 to 200
Outputs:
- block_out: bfloat16 [8192, 7168], P('req', 'tensor')
The draws below stay inside these ranges and needn't reach their ends.
Inputs may be any that keep to these rules, and one draw needn't show every extreme that they name: `prompt_length`: some request in every draw fills all 128 rows of its block. `cache_length`: some cache in every draw has 2048 positions. `page_slot_table`: each row is a permutation of the cached requests over the pool slots of one device.
All inputs are finite; a program needn't handle non-finite values.
Results may differ from the reference program's by a relative error of at most 0.035.
Values may be sent and summed in bfloat16 or wider, within the bound.
No kernel may reach another device: no remote copies, remote signals or barrier semaphores. Data moves between devices by JAX's collectives and lax.ppermute only.
A program may use at most 128 MiB of HBM per device.

```python
import math
import jax
import jax.numpy as jnp
import numpy as np
from jax import lax

MODEL_WIDTH = 7168
HEAD_SIZE = 128
KEY_VALUE_HEADS = 8
QUERY_HEADS = 32
ADAPTER_RANK = 16
SLOT = 128
PAGE = 128
TOKEN_ROWS = 8192
REQUESTS = 64
CACHED = 32
CACHE = 2048
ADAPTER_COUNT = 64
N_REQ = 16
N_TENSOR = 8


def draw_prompt_length(key, part):
    drawn_values = jax.random.randint(key, (REQUESTS,), SLOT // 4, SLOT + 1)
    picked = jax.random.randint(jax.random.fold_in(key, 11), (), 0, REQUESTS)
    return drawn_values.at[picked].set(SLOT).astype(jnp.int32)


def draw_cache_length(key, part):
    drawn_values = jax.random.randint(key, (CACHED,), PAGE // 8, CACHE + 1)
    picked = jax.random.randint(jax.random.fold_in(key, 13), (), 0, CACHED)
    return drawn_values.at[picked].set(CACHE).astype(jnp.int32)


def draw_page_slot_table(key, part):
    row_keys = jax.random.split(key, N_REQ)
    return jax.vmap(lambda row_key: jax.random.permutation(row_key, CACHED))(row_keys).astype(jnp.int32)


def draw_cache_page_pool(key, part):
    lead_shape = (N_REQ * CACHED, PAGE, KEY_VALUE_HEADS, HEAD_SIZE)
    key_part = jax.random.fold_in(key, 21)
    value_part = jax.random.fold_in(key, 22)
    key_entries = jnp.clip(jax.random.normal(key_part, lead_shape, jnp.float32) * 1.4142135, -8.5, 8.5)
    value_entries = jnp.clip(jax.random.normal(value_part, lead_shape, jnp.float32), -6.0, 6.0)
    joined = jnp.concatenate([key_entries, value_entries], axis=-1)
    return joined.reshape(N_REQ * CACHED, PAGE, KEY_VALUE_HEADS * 2 * HEAD_SIZE).astype(jnp.bfloat16)


def set_ends(array, own_key, smallest, top_value):
    dims = array.shape
    place = [jax.random.randint(jax.random.fold_in(own_key, axis), (), 0, dims[axis]) for axis in range(len(dims))]
    array = array.at[tuple(place)].set(smallest)
    longest = dims.index(max(dims))
    place[longest] = (place[longest] + 1) % dims[longest]
    return array.at[tuple(place)].set(top_value)


def level_of(own_key, extent, pieces, low, largest):
    def one(dim, shards_of):
        draws = jax.random.uniform(jax.random.fold_in(jax.random.fold_in(own_key, 6), dim), (shards_of,), jnp.float32, low / len(pieces), largest / len(pieces))
        return jnp.repeat(jnp.exp(draws), extent[dim] // shards_of).reshape((-1,) + (1,) * (len(extent) - dim - 1))

    loudness = one(*pieces[0])
    for cut in pieces[1:]:
        loudness = loudness * one(*cut)
    return loudness


def rank_table(count, lean):
    weights = [(1 << 20) // math.isqrt(standing ** lean) + 1 for standing in range(1, count + 1)]
    spread = 1 + sum(weights) // (1 << 30)
    return np.cumsum(np.array([max(1, weight // spread) for weight in weights]))


def skewed_ids(own_key, shape, amount, skew):
    grid = rank_table(amount, skew)
    pick = jax.random.randint(jax.random.fold_in(own_key, 1), shape, 0, int(grid[amount - 1]))
    rank = jnp.searchsorted(jnp.asarray(grid, jnp.int32), pick, side="right")
    return jax.random.permutation(jax.random.fold_in(own_key, 2), amount)[rank].astype(jnp.int32)


def centred(key, dims, spread, reach, cuts=(), kind=jnp.bfloat16):
    factor_of = level_of(key, dims, cuts, -0.22, 0.18) if cuts else 1.0
    values = jax.random.normal(key, dims, jnp.float32) * spread * factor_of
    return jnp.minimum(jnp.maximum(values, -reach), reach).astype(kind)


def setup_inputs(seed: int = 0) -> dict:
    splits = jax.random.split(jax.random.key(seed), 17)
    residual_input = centred(splits[0], (TOKEN_ROWS, MODEL_WIDTH), 1.0, 6.0, ((0, 16), (1, 8)))
    input_norm_gain = jnp.clip(1.0 + 0.15 * jax.random.normal(splits[1], (MODEL_WIDTH,), jnp.float32), 0.25, 1.75)
    query_weight = centred(splits[2], (MODEL_WIDTH, QUERY_HEADS * HEAD_SIZE), (MODEL_WIDTH // 2) ** -0.5, 0.09375, ((1, 8),))
    key_value_weight = centred(splits[3], (MODEL_WIDTH, 2 * KEY_VALUE_HEADS * HEAD_SIZE), (MODEL_WIDTH // 2) ** -0.5, 0.09375, ((1, 8),))
    output_weight = centred(splits[4], (QUERY_HEADS * HEAD_SIZE, MODEL_WIDTH), (QUERY_HEADS * HEAD_SIZE // 16) ** -0.5, 0.375, ((0, 8),))
    adapter_down_maps = centred(splits[5], (ADAPTER_COUNT, 3 * ADAPTER_RANK, MODEL_WIDTH), MODEL_WIDTH ** -0.5, 0.0625, ((0, 16), (2, 8)))
    adapter_query_up = centred(splits[6], (ADAPTER_COUNT, ADAPTER_RANK, QUERY_HEADS * HEAD_SIZE), (16 * ADAPTER_RANK) ** -0.5, 0.375, ((0, 16), (2, 8)))
    adapter_key_value_up = centred(splits[7], (ADAPTER_COUNT, 2, ADAPTER_RANK, KEY_VALUE_HEADS * HEAD_SIZE), (16 * ADAPTER_RANK) ** -0.5, 0.375, ((0, 16), (3, 8)))
    adapter_output_down = centred(splits[8], (ADAPTER_COUNT, ADAPTER_RANK, QUERY_HEADS * HEAD_SIZE), (QUERY_HEADS * HEAD_SIZE // 16) ** -0.5, 0.375, ((0, 16), (2, 8)))
    adapter_output_up = centred(splits[9], (ADAPTER_COUNT, ADAPTER_RANK, MODEL_WIDTH), (16 * ADAPTER_RANK) ** -0.5, 0.375, ((0, 16), (2, 8)))
    request_adapter = set_ends(skewed_ids(splits[10], (REQUESTS,), ADAPTER_COUNT, 2), jax.random.fold_in(splits[10], 3), 0, ADAPTER_COUNT - 1).astype(jnp.int32)
    prompt_length = draw_prompt_length(jax.random.fold_in(splits[16], 71), 0)
    cache_length = draw_cache_length(jax.random.fold_in(splits[16], 71), 0)
    first_page_device = set_ends(jax.random.randint(splits[13], (CACHED,), 0, N_REQ), jax.random.fold_in(splits[13], 1), 0, N_REQ - 1).astype(jnp.int32)
    page_slot_table = draw_page_slot_table(jax.random.fold_in(splits[16], 71), 0)
    cache_page_pool = draw_cache_page_pool(jax.random.fold_in(splits[16], 71), 0)
    return dict(residual_input=residual_input, input_norm_gain=input_norm_gain, query_weight=query_weight, key_value_weight=key_value_weight, output_weight=output_weight, adapter_down_maps=adapter_down_maps, adapter_query_up=adapter_query_up, adapter_key_value_up=adapter_key_value_up, adapter_output_down=adapter_output_down, adapter_output_up=adapter_output_up, request_adapter=request_adapter, prompt_length=prompt_length, cache_length=cache_length, first_page_device=first_page_device, page_slot_table=page_slot_table, cache_page_pool=cache_page_pool)


ROPE_BASE = 5000000.0
ADAPTER_SCALE = 2.0
EPSILON = 1e-05
NEG_FILL = -1e+30

def rotate(vectors, positions):
    half_dim = vectors.shape[-1] // 2
    frequency = ROPE_BASE ** (-jnp.arange(half_dim, dtype=jnp.float32) / half_dim)
    angles = positions.astype(jnp.float32)[..., None] * frequency
    cosine = jnp.cos(angles)
    sine_part = jnp.sin(angles)
    front_half = vectors[..., :half_dim]
    back_half = vectors[..., half_dim:]
    return jnp.concatenate([front_half * cosine - back_half * sine_part, back_half * cosine + front_half * sine_part], axis=-1)

def reference(residual_input, input_norm_gain, query_weight, key_value_weight, output_weight, adapter_down_maps, adapter_query_up, adapter_key_value_up, adapter_output_down, adapter_output_up, request_adapter, prompt_length, cache_length, first_page_device, page_slot_table, cache_page_pool):
    group_size = QUERY_HEADS // KEY_VALUE_HEADS
    widened = residual_input.astype(jnp.float32)
    inverse = lax.rsqrt(lax.optimization_barrier(jnp.mean(widened * widened, axis=1, keepdims=True)) + EPSILON)
    normed = lax.optimization_barrier((widened * inverse * input_norm_gain).astype(jnp.bfloat16))
    by_request = normed.reshape(REQUESTS, SLOT, MODEL_WIDTH).astype(jnp.float32)
    down_picked = adapter_down_maps[request_adapter].astype(jnp.float32)
    reduced_input = jnp.einsum('rsd,rkd->rsk', by_request, down_picked).astype(jnp.bfloat16)
    reduced_input = lax.optimization_barrier(reduced_input).astype(jnp.float32)
    query_picked = adapter_query_up[request_adapter].astype(jnp.float32)
    query_rows = jnp.dot(normed, query_weight, preferred_element_type=jnp.float32).reshape(REQUESTS, SLOT, QUERY_HEADS * HEAD_SIZE)
    query_rows = query_rows + ADAPTER_SCALE * jnp.einsum('ibm,imf->ibf', reduced_input[..., :ADAPTER_RANK], query_picked)
    keyval = jnp.dot(normed, key_value_weight, preferred_element_type=jnp.float32).reshape(REQUESTS, SLOT, KEY_VALUE_HEADS, 2 * HEAD_SIZE)
    key_value_picked = adapter_key_value_up[request_adapter].astype(jnp.float32)
    key_add = jnp.einsum('ibm,imf->ibf', reduced_input[..., ADAPTER_RANK:2 * ADAPTER_RANK], key_value_picked[:, 0]).reshape(REQUESTS, SLOT, KEY_VALUE_HEADS, HEAD_SIZE)
    value_add = jnp.einsum('ibm,imf->ibf', reduced_input[..., 2 * ADAPTER_RANK:], key_value_picked[:, 1]).reshape(REQUESTS, SLOT, KEY_VALUE_HEADS, HEAD_SIZE)
    offsets = jnp.stack([jnp.zeros_like(cache_length), cache_length], axis=1).reshape(REQUESTS)
    positions = offsets[:, None] + jnp.arange(SLOT, dtype=jnp.int32)[None, :]
    query_rot = rotate(query_rows.reshape(REQUESTS, SLOT, KEY_VALUE_HEADS, group_size, HEAD_SIZE), positions[:, :, None, None]).astype(jnp.bfloat16)
    key_rot = rotate(keyval[..., :HEAD_SIZE] + key_add, positions[:, :, None]).astype(jnp.bfloat16)
    value_new = (keyval[..., HEAD_SIZE:] + value_add).astype(jnp.bfloat16)
    holder_of = (first_page_device[:, None] + jnp.arange(N_REQ, dtype=jnp.int32)[None, :]) % N_REQ
    pool_rows = holder_of * CACHED + page_slot_table[holder_of, jnp.arange(CACHED, dtype=jnp.int32)[:, None]]
    slot_index = jnp.arange(SLOT, dtype=jnp.int32)
    cache_index = jnp.arange(CACHE, dtype=jnp.int32)

    def one_request(request):
        cached = request // 2
        cache_limit = jnp.where(request % 2 == 1, cache_length[cached], 0)
        page_block = cache_page_pool[pool_rows[cached]].reshape(CACHE, KEY_VALUE_HEADS, 2 * HEAD_SIZE)
        key_rows = jnp.concatenate([page_block[..., :HEAD_SIZE], key_rot[request]], axis=0).astype(jnp.float32)
        value_rows = jnp.concatenate([page_block[..., HEAD_SIZE:], value_new[request]], axis=0).astype(jnp.float32)
        length = prompt_length[request]
        cache_mask = jnp.broadcast_to((cache_index < cache_limit)[None, :], (SLOT, CACHE))
        own_mask = (slot_index[None, :] <= slot_index[:, None]) & (slot_index[None, :] < length)
        allowed = jnp.concatenate([cache_mask, own_mask], axis=1)[None, :, None, :]
        scores = jnp.einsum('svgd,kvd->vsgk', query_rot[request].astype(jnp.float32), key_rows) * HEAD_SIZE ** (-0.5)
        scores = jnp.where(allowed, scores, NEG_FILL)
        peak_scores = lax.optimization_barrier(jnp.max(scores, axis=-1, keepdims=True))
        weights = jnp.where(allowed, jnp.exp(scores - peak_scores), 0.0)
        totals = lax.optimization_barrier(jnp.sum(weights, axis=-1))
        rounded = lax.optimization_barrier(weights.astype(jnp.bfloat16)).astype(jnp.float32)
        summed = jnp.einsum('vsgk,kvd->svgd', rounded, value_rows)
        result = summed / jnp.transpose(totals, (1, 0, 2))[..., None]
        result = jnp.where((slot_index < length)[:, None, None, None], result, 0.0)
        return result.reshape(SLOT, QUERY_HEADS * HEAD_SIZE).astype(jnp.bfloat16)
    attended = lax.map(one_request, jnp.arange(REQUESTS, dtype=jnp.int32))
    attended = lax.optimization_barrier(attended.reshape(TOKEN_ROWS, QUERY_HEADS * HEAD_SIZE))
    head_width = QUERY_HEADS * HEAD_SIZE // N_TENSOR
    head_total = jnp.zeros((TOKEN_ROWS, MODEL_WIDTH), jnp.float32)
    for part_index in range(N_TENSOR):
        head_term = jnp.dot(attended[:, part_index * head_width:(part_index + 1) * head_width], output_weight[part_index * head_width:(part_index + 1) * head_width], preferred_element_type=jnp.float32).astype(jnp.bfloat16)
        head_total = head_total + lax.optimization_barrier(head_term).astype(jnp.float32)
    output_down_picked = adapter_output_down[request_adapter].astype(jnp.float32)
    reduced_output = jnp.einsum('rsc,rkc->rsk', attended.reshape(REQUESTS, SLOT, QUERY_HEADS * HEAD_SIZE).astype(jnp.float32), output_down_picked).astype(jnp.bfloat16)
    reduced_output = lax.optimization_barrier(reduced_output).astype(jnp.float32)
    adapter_output = jnp.einsum('ibm,imf->ibf', reduced_output, adapter_output_up[request_adapter].astype(jnp.float32)).reshape(TOKEN_ROWS, MODEL_WIDTH)
    return (head_total + ADAPTER_SCALE * adapter_output).astype(jnp.bfloat16)
```

```python
import jax
import jax.numpy as jnp
from jax import lax
from jax.sharding import PartitionSpec as P

HEAD_SIZE = 128


ROPE_BASE = 5000000.0
ADAPTER_SCALE = 2.0
EPSILON = 1e-05
NEG_FILL = -1e30


def rotate(vectors, positions):
    half_dim = vectors.shape[-1] // 2
    frequency = ROPE_BASE ** (-jnp.arange(half_dim, dtype=jnp.float32) / half_dim)
    angles = positions.astype(jnp.float32)[..., None] * frequency
    cosine = jnp.cos(angles)
    sine_part = jnp.sin(angles)
    front_half = vectors[..., :half_dim]
    back_half = vectors[..., half_dim:]
    return jnp.concatenate(
        [front_half * cosine - back_half * sine_part, back_half * cosine + front_half * sine_part],
        axis=-1,
    )


def partial_softmax(query_rows, key_rows, value_rows, allowed):
    score_scale = query_rows.shape[-1] ** (-0.5)
    scores = (
        jnp.einsum("bsvgd,bkvd->bvsgk", query_rows, key_rows, preferred_element_type=jnp.float32)
        * score_scale
    )
    spread_mask = allowed[:, None, :, None, :]
    scores = jnp.where(spread_mask, scores, NEG_FILL)
    peak_scores = jnp.max(scores, axis=-1)
    weights = jnp.where(spread_mask, jnp.exp(scores - peak_scores[..., None]), 0.0)
    totals = jnp.sum(weights, axis=-1)
    summed = jnp.einsum(
        "bvsgk,bkvd->bvsgd",
        weights.astype(jnp.bfloat16),
        value_rows,
        preferred_element_type=jnp.float32,
    )
    return (peak_scores, totals, summed)


def gather_by_exchange(piece, axis_name, count):
    spread = jnp.broadcast_to(piece[None], (count,) + piece.shape)
    return lax.all_to_all(spread, axis_name, split_axis=0, concat_axis=0, tiled=True)


def local(
    residual_input,
    input_norm_gain,
    query_weight,
    key_value_weight,
    output_weight,
    adapter_down_maps,
    adapter_query_up,
    adapter_key_value_up,
    adapter_output_down,
    adapter_output_up,
    request_adapter,
    prompt_length,
    cache_length,
    first_page_device,
    page_slot_table,
    cache_page_pool,
):
    holders = lax.axis_size("req")
    req_index = lax.axis_index("req")
    tensor_index = lax.axis_index("tensor")
    request_number = request_adapter.shape[0]
    cached_count = request_number // 2
    row_count = residual_input.shape[0]
    request_slot_rows = row_count // request_number
    piece_width = residual_input.shape[1]
    local_kv = key_value_weight.shape[1] // (2 * HEAD_SIZE)
    group_size = query_weight.shape[1] // (HEAD_SIZE * local_kv)
    page_rows = cache_page_pool.shape[1]
    tensor_count = lax.axis_size("tensor")
    gathered = gather_by_exchange(residual_input, "tensor", tensor_count)
    widened = gathered.astype(jnp.float32)
    inverse = lax.rsqrt(
        jnp.sum(widened * widened, axis=(0, 2), keepdims=True) / (tensor_count * piece_width)
        + EPSILON
    )
    gain_parts = input_norm_gain.reshape(tensor_count, 1, piece_width)
    normed_parts = (widened * inverse * gain_parts).astype(jnp.bfloat16)
    adapter_parts = (
        adapter_down_maps,
        adapter_query_up,
        adapter_key_value_up,
        adapter_output_down,
        adapter_output_up,
    )
    local_adapters = adapter_down_maps.shape[0]
    flat_parts = [part.reshape(local_adapters, -1) for part in adapter_parts]
    joined = jnp.concatenate(flat_parts, axis=1)
    every_adapter = gather_by_exchange(joined, "req", holders).reshape(
        holders * local_adapters, joined.shape[1]
    )
    picked = jnp.take(every_adapter, request_adapter, axis=0, mode="clip")
    picked_parts = []
    start = 0
    for part, flat in zip(adapter_parts, flat_parts):
        width = flat.shape[1]
        picked_parts.append(
            picked[:, start : start + width].reshape((request_number,) + part.shape[1:])
        )
        start += width
    down_picked, query_picked, key_value_picked, output_down_picked, oup_sel = picked_parts
    adapter_rank_size = query_picked.shape[1]
    own_columns = lax.dynamic_index_in_dim(normed_parts, tensor_index, 0, keepdims=False).reshape(
        request_number, request_slot_rows, piece_width
    )
    partial_low = jnp.einsum(
        "rsd,rkd->rsk", own_columns, down_picked, preferred_element_type=jnp.float32
    )
    reduced_input = (
        gather_by_exchange(partial_low.astype(jnp.bfloat16), "tensor", tensor_count)
        .astype(jnp.float32)
        .sum(axis=0)
        .astype(jnp.bfloat16)
    )
    query_rows = jnp.einsum(
        "tsf,tfc->sc",
        normed_parts,
        query_weight.reshape(tensor_count, piece_width, -1),
        preferred_element_type=jnp.float32,
    ).reshape(request_number, request_slot_rows, -1)
    query_rows = query_rows + ADAPTER_SCALE * jnp.einsum(
        "ibm,imf->ibf",
        reduced_input[..., :adapter_rank_size],
        query_picked,
        preferred_element_type=jnp.float32,
    )
    keyval = jnp.einsum(
        "tsf,tfc->sc",
        normed_parts,
        key_value_weight.reshape(tensor_count, piece_width, -1),
        preferred_element_type=jnp.float32,
    ).reshape(
        request_number, request_slot_rows, local_kv, 2 * HEAD_SIZE
    )
    key_add = jnp.einsum(
        "ibm,imf->ibf",
        reduced_input[..., adapter_rank_size : 2 * adapter_rank_size],
        key_value_picked[:, 0],
        preferred_element_type=jnp.float32,
    ).reshape(request_number, request_slot_rows, local_kv, HEAD_SIZE)
    value_add = jnp.einsum(
        "ibm,imf->ibf",
        reduced_input[..., 2 * adapter_rank_size :],
        key_value_picked[:, 1],
        preferred_element_type=jnp.float32,
    ).reshape(request_number, request_slot_rows, local_kv, HEAD_SIZE)
    my_cache = lax.dynamic_slice_in_dim(cache_length, req_index * cached_count, cached_count, 0)
    offsets = jnp.stack([jnp.zeros_like(my_cache), my_cache], axis=1).reshape(request_number)
    slot_index = jnp.arange(request_slot_rows, dtype=jnp.int32)
    positions = offsets[:, None] + slot_index[None, :]
    query_rot = rotate(
        query_rows.reshape(request_number, request_slot_rows, local_kv, group_size, HEAD_SIZE),
        positions[:, :, None, None],
    ).astype(jnp.bfloat16)
    key_rot = rotate(keyval[..., :HEAD_SIZE] + key_add, positions[:, :, None]).astype(jnp.bfloat16)
    value_new = (keyval[..., HEAD_SIZE:] + value_add).astype(jnp.bfloat16)
    causal = slot_index[None, :, None] >= slot_index[None, None, :]
    own_mask = causal & (slot_index[None, None, :] < prompt_length[:, None, None])
    own_part = partial_softmax(query_rot, key_rot, value_new, own_mask)
    asked_queries = query_rot[1::2]
    slot_order = page_slot_table[0].reshape(holders, cached_count).T.reshape(-1)
    outgoing = cache_page_pool[slot_order].reshape(
        cached_count, holders, page_rows, cache_page_pool.shape[2]
    )
    arrived = lax.all_to_all(outgoing, "req", split_axis=1, concat_axis=1, tiled=True)
    my_base = lax.dynamic_slice_in_dim(first_page_device, req_index * cached_count, cached_count, 0)
    page_of = (jnp.arange(holders, dtype=jnp.int32)[None, :] - my_base[:, None]) % holders
    key_pos = (
        page_of[:, :, None] * page_rows + jnp.arange(page_rows, dtype=jnp.int32)[None, None, :]
    ).reshape(cached_count, holders * page_rows)
    entries = arrived.reshape(cached_count, holders * page_rows, local_kv, 2 * HEAD_SIZE)
    visible = jnp.broadcast_to(
        (key_pos < my_cache[:, None])[:, None, :],
        (cached_count, request_slot_rows, holders * page_rows),
    )
    cache_part = partial_softmax(
        asked_queries, entries[..., :HEAD_SIZE], entries[..., HEAD_SIZE:], visible
    )
    filler = jnp.full_like(cache_part[0], NEG_FILL)
    spread_peak = jnp.stack([filler, cache_part[0]], axis=1).reshape(own_part[0].shape)
    spread_total = jnp.stack([jnp.zeros_like(cache_part[1]), cache_part[1]], axis=1).reshape(
        own_part[1].shape
    )
    spread_sum = jnp.stack([jnp.zeros_like(cache_part[2]), cache_part[2]], axis=1).reshape(
        own_part[2].shape
    )
    highest_all = jnp.maximum(own_part[0], spread_peak)
    own_weight = jnp.exp(own_part[0] - highest_all)
    cache_weight = jnp.exp(spread_peak - highest_all)
    denominator = own_part[1] * own_weight + spread_total * cache_weight
    numerator = own_part[2] * own_weight[..., None] + spread_sum * cache_weight[..., None]
    live_rows = slot_index[None, :] < prompt_length[:, None]
    attended = jnp.where(
        live_rows[:, None, :, None, None], numerator / denominator[..., None], 0.0
    ).astype(jnp.bfloat16)
    attended = jnp.transpose(attended, (0, 2, 1, 3, 4)).reshape(row_count, -1)
    head_terms = jnp.einsum(
        "sc,ctf->tsf",
        attended,
        output_weight.reshape(output_weight.shape[0], tensor_count, piece_width),
        preferred_element_type=jnp.float32,
    )
    low_part = jnp.einsum(
        "rsc,rkc->rsk",
        attended.reshape(request_number, request_slot_rows, -1),
        output_down_picked,
        preferred_element_type=jnp.float32,
    )
    reduced_output = (
        gather_by_exchange(low_part.astype(jnp.bfloat16), "tensor", tensor_count)
        .astype(jnp.float32)
        .sum(axis=0)
        .astype(jnp.bfloat16)
    )
    head_total = (
        lax.all_to_all(
            head_terms.astype(jnp.bfloat16), "tensor", split_axis=0, concat_axis=0, tiled=True
        )
        .astype(jnp.float32)
        .sum(axis=0)
    )
    adapter_output = jnp.einsum(
        "ibm,imf->ibf", reduced_output, oup_sel, preferred_element_type=jnp.float32
    ).reshape(row_count, -1)
    return (head_total + ADAPTER_SCALE * adapter_output).astype(jnp.bfloat16)


def solution(mesh):
    placed = (
        P("req", "tensor"),
        P(),
        P(None, "tensor"),
        P(None, "tensor"),
        P("tensor", None),
        P("req", None, "tensor"),
        P("req", None, "tensor"),
        P("req", None, None, "tensor"),
        P("req", None, "tensor"),
        P("req", None, "tensor"),
        P("req"),
        P("req"),
        P(),
        P(),
        P("req", None),
        P("req", None, "tensor"),
    )
    return jax.shard_map(
        local, mesh=mesh, in_specs=placed, out_specs=P("req", "tensor"), check_vma=False
    )
```

```python
import jax
import jax.numpy as jnp
from jax import lax
from jax.sharding import PartitionSpec as P

HEAD_SIZE = 128


ROPE_BASE = 5000000.0
ADAPTER_SCALE = 2.0
EPSILON = 1e-05
NEG_FILL = -1e30


def rotate(vectors, positions):
    half_dim = vectors.shape[-1] // 2
    frequency = ROPE_BASE ** (-jnp.arange(half_dim, dtype=jnp.float32) / half_dim)
    angles = positions.astype(jnp.float32)[..., None] * frequency
    cosine = jnp.cos(angles)
    sine_part = jnp.sin(angles)
    front_half = vectors[..., :half_dim]
    back_half = vectors[..., half_dim:]
    return jnp.concatenate(
        [front_half * cosine - back_half * sine_part, back_half * cosine + front_half * sine_part],
        axis=-1,
    )


def partial_softmax(query_rows, key_rows, value_rows, allowed):
    score_scale = query_rows.shape[-1] ** (-0.5)
    scores = (
        jnp.einsum("bsvgd,bkvd->bvsgk", query_rows, key_rows, preferred_element_type=jnp.float32)
        * score_scale
    )
    spread_mask = allowed[:, None, :, None, :]
    scores = jnp.where(spread_mask, scores, NEG_FILL)
    peak_scores = jnp.max(scores, axis=-1)
    weights = jnp.where(spread_mask, jnp.exp(scores - peak_scores[..., None]), 0.0)
    totals = jnp.sum(weights, axis=-1)
    summed = jnp.einsum(
        "bvsgk,bkvd->bvsgd",
        weights.astype(jnp.bfloat16),
        value_rows,
        preferred_element_type=jnp.float32,
    )
    return (peak_scores, totals, summed)


def gather_by_exchange(piece, axis_name, count):
    spread = jnp.broadcast_to(piece[None], (count,) + piece.shape)
    return lax.all_to_all(spread, axis_name, split_axis=0, concat_axis=0, tiled=True)


def local(
    residual_input,
    input_norm_gain,
    query_weight,
    key_value_weight,
    output_weight,
    adapter_down_maps,
    adapter_query_up,
    adapter_key_value_up,
    adapter_output_down,
    adapter_output_up,
    request_adapter,
    prompt_length,
    cache_length,
    first_page_device,
    page_slot_table,
    cache_page_pool,
):
    holders = lax.axis_size("req")
    req_index = lax.axis_index("req")
    tensor_index = lax.axis_index("tensor")
    request_number = request_adapter.shape[0]
    cached_count = request_number // 2
    row_count = residual_input.shape[0]
    request_slot_rows = row_count // request_number
    piece_width = residual_input.shape[1]
    local_kv = key_value_weight.shape[1] // (2 * HEAD_SIZE)
    group_size = query_weight.shape[1] // (HEAD_SIZE * local_kv)
    page_rows = cache_page_pool.shape[1]
    tensor_count = lax.axis_size("tensor")
    gathered = lax.all_gather(residual_input, "tensor", axis=0, tiled=False)
    widened = gathered.astype(jnp.float32)
    inverse = lax.rsqrt(
        jnp.sum(widened * widened, axis=(0, 2), keepdims=True) / (tensor_count * piece_width)
        + EPSILON
    )
    gain_parts = input_norm_gain.reshape(tensor_count, 1, piece_width)
    normed_parts = (widened * inverse * gain_parts).astype(jnp.bfloat16)
    adapter_parts = (
        adapter_down_maps,
        adapter_query_up,
        adapter_key_value_up,
        adapter_output_down,
        adapter_output_up,
    )
    local_adapters = adapter_down_maps.shape[0]
    flat_parts = [part.reshape(local_adapters, -1) for part in adapter_parts]
    joined = jnp.concatenate(flat_parts, axis=1)
    every_adapter = lax.all_gather(joined, "req", axis=0, tiled=False).reshape(
        holders * local_adapters, joined.shape[1]
    )
    picked = jnp.take(every_adapter, request_adapter, axis=0, mode="clip")
    picked_parts = []
    start = 0
    for part, flat in zip(adapter_parts, flat_parts):
        width = flat.shape[1]
        picked_parts.append(
            picked[:, start : start + width].reshape((request_number,) + part.shape[1:])
        )
        start += width
    down_picked, query_picked, key_value_picked, output_down_picked, oup_sel = picked_parts
    adapter_rank_size = query_picked.shape[1]
    own_columns = lax.dynamic_index_in_dim(normed_parts, tensor_index, 0, keepdims=False).reshape(
        request_number, request_slot_rows, piece_width
    )
    partial_low = jnp.einsum(
        "rsd,rkd->rsk", own_columns, down_picked, preferred_element_type=jnp.float32
    )
    reduced_input = (
        gather_by_exchange(partial_low.astype(jnp.bfloat16), "tensor", tensor_count)
        .astype(jnp.float32)
        .sum(axis=0)
        .astype(jnp.bfloat16)
    )
    query_rows = jnp.einsum(
        "tsf,tfc->sc",
        normed_parts,
        query_weight.reshape(tensor_count, piece_width, -1),
        preferred_element_type=jnp.float32,
    ).reshape(request_number, request_slot_rows, -1)
    query_rows = query_rows + ADAPTER_SCALE * jnp.einsum(
        "ibm,imf->ibf",
        reduced_input[..., :adapter_rank_size],
        query_picked,
        preferred_element_type=jnp.float32,
    )
    keyval = jnp.einsum(
        "tsf,tfc->sc",
        normed_parts,
        key_value_weight.reshape(tensor_count, piece_width, -1),
        preferred_element_type=jnp.float32,
    ).reshape(
        request_number, request_slot_rows, local_kv, 2 * HEAD_SIZE
    )
    key_add = jnp.einsum(
        "ibm,imf->ibf",
        reduced_input[..., adapter_rank_size : 2 * adapter_rank_size],
        key_value_picked[:, 0],
        preferred_element_type=jnp.float32,
    ).reshape(request_number, request_slot_rows, local_kv, HEAD_SIZE)
    value_add = jnp.einsum(
        "ibm,imf->ibf",
        reduced_input[..., 2 * adapter_rank_size :],
        key_value_picked[:, 1],
        preferred_element_type=jnp.float32,
    ).reshape(request_number, request_slot_rows, local_kv, HEAD_SIZE)
    my_cache = lax.dynamic_slice_in_dim(cache_length, req_index * cached_count, cached_count, 0)
    offsets = jnp.stack([jnp.zeros_like(my_cache), my_cache], axis=1).reshape(request_number)
    slot_index = jnp.arange(request_slot_rows, dtype=jnp.int32)
    positions = offsets[:, None] + slot_index[None, :]
    query_rot = rotate(
        query_rows.reshape(request_number, request_slot_rows, local_kv, group_size, HEAD_SIZE),
        positions[:, :, None, None],
    ).astype(jnp.bfloat16)
    key_rot = rotate(keyval[..., :HEAD_SIZE] + key_add, positions[:, :, None]).astype(jnp.bfloat16)
    value_new = (keyval[..., HEAD_SIZE:] + value_add).astype(jnp.bfloat16)
    causal = slot_index[None, :, None] >= slot_index[None, None, :]
    own_mask = causal & (slot_index[None, None, :] < prompt_length[:, None, None])
    own_part = partial_softmax(query_rot, key_rot, value_new, own_mask)
    asked_queries = query_rot[1::2]
    slot_order = page_slot_table[0].reshape(holders, cached_count).T.reshape(-1)
    outgoing = cache_page_pool[slot_order].reshape(
        cached_count, holders, page_rows, cache_page_pool.shape[2]
    )
    arrived = lax.all_to_all(outgoing, "req", split_axis=1, concat_axis=1, tiled=True)
    my_base = lax.dynamic_slice_in_dim(first_page_device, req_index * cached_count, cached_count, 0)
    page_of = (jnp.arange(holders, dtype=jnp.int32)[None, :] - my_base[:, None]) % holders
    key_pos = (
        page_of[:, :, None] * page_rows + jnp.arange(page_rows, dtype=jnp.int32)[None, None, :]
    ).reshape(cached_count, holders * page_rows)
    entries = arrived.reshape(cached_count, holders * page_rows, local_kv, 2 * HEAD_SIZE)
    visible = jnp.broadcast_to(
        (key_pos < my_cache[:, None])[:, None, :],
        (cached_count, request_slot_rows, holders * page_rows),
    )
    cache_part = partial_softmax(
        asked_queries, entries[..., :HEAD_SIZE], entries[..., HEAD_SIZE:], visible
    )
    filler = jnp.full_like(cache_part[0], NEG_FILL)
    spread_peak = jnp.stack([filler, cache_part[0]], axis=1).reshape(own_part[0].shape)
    spread_total = jnp.stack([jnp.zeros_like(cache_part[1]), cache_part[1]], axis=1).reshape(
        own_part[1].shape
    )
    spread_sum = jnp.stack([jnp.zeros_like(cache_part[2]), cache_part[2]], axis=1).reshape(
        own_part[2].shape
    )
    highest_all = jnp.maximum(own_part[0], spread_peak)
    own_weight = jnp.exp(own_part[0] - highest_all)
    cache_weight = jnp.exp(spread_peak - highest_all)
    denominator = own_part[1] * own_weight + spread_total * cache_weight
    numerator = own_part[2] * own_weight[..., None] + spread_sum * cache_weight[..., None]
    live_rows = slot_index[None, :] < prompt_length[:, None]
    attended = jnp.where(
        live_rows[:, None, :, None, None], numerator / denominator[..., None], 0.0
    ).astype(jnp.bfloat16)
    attended = jnp.transpose(attended, (0, 2, 1, 3, 4)).reshape(row_count, -1)
    head_terms = jnp.einsum(
        "sc,ctf->tsf",
        attended,
        output_weight.reshape(output_weight.shape[0], tensor_count, piece_width),
        preferred_element_type=jnp.float32,
    )
    low_part = jnp.einsum(
        "rsc,rkc->rsk",
        attended.reshape(request_number, request_slot_rows, -1),
        output_down_picked,
        preferred_element_type=jnp.float32,
    )
    reduced_output = (
        gather_by_exchange(low_part.astype(jnp.bfloat16), "tensor", tensor_count)
        .astype(jnp.float32)
        .sum(axis=0)
        .astype(jnp.bfloat16)
    )
    head_total = lax.psum_scatter(
        head_terms.astype(jnp.bfloat16), "tensor", scatter_dimension=0, tiled=False
    ).astype(jnp.float32)
    adapter_output = jnp.einsum(
        "ibm,imf->ibf", reduced_output, oup_sel, preferred_element_type=jnp.float32
    ).reshape(row_count, -1)
    return (head_total + ADAPTER_SCALE * adapter_output).astype(jnp.bfloat16)


def solution(mesh):
    placed = (
        P("req", "tensor"),
        P(),
        P(None, "tensor"),
        P(None, "tensor"),
        P("tensor", None),
        P("req", None, "tensor"),
        P("req", None, "tensor"),
        P("req", None, None, "tensor"),
        P("req", None, "tensor"),
        P("req", None, "tensor"),
        P("req"),
        P("req"),
        P(),
        P(),
        P("req", None),
        P("req", None, "tensor"),
    )
    return jax.shard_map(
        local, mesh=mesh, in_specs=placed, out_specs=P("req", "tensor"), check_vma=False
    )
```

```python
import jax
import jax.numpy as jnp
from jax import lax
from jax.sharding import PartitionSpec as P

HEAD_SIZE = 128


ROPE_BASE = 5000000.0
ADAPTER_SCALE = 2.0
EPSILON = 1e-05
NEG_FILL = -1e30


def rotate(vectors, positions):
    half_dim = vectors.shape[-1] // 2
    frequency = ROPE_BASE ** (-jnp.arange(half_dim, dtype=jnp.float32) / half_dim)
    angles = positions.astype(jnp.float32)[..., None] * frequency
    cosine = jnp.cos(angles)
    sine_part = jnp.sin(angles)
    front_half = vectors[..., :half_dim]
    back_half = vectors[..., half_dim:]
    return jnp.concatenate(
        [front_half * cosine - back_half * sine_part, back_half * cosine + front_half * sine_part],
        axis=-1,
    )


def partial_softmax(query_rows, key_rows, value_rows, allowed):
    score_scale = query_rows.shape[-1] ** (-0.5)
    scores = (
        jnp.einsum("bsvgd,bkvd->bvsgk", query_rows, key_rows, preferred_element_type=jnp.float32)
        * score_scale
    )
    spread_mask = allowed[:, None, :, None, :]
    scores = jnp.where(spread_mask, scores, NEG_FILL)
    peak_scores = jnp.max(scores, axis=-1)
    weights = jnp.where(spread_mask, jnp.exp(scores - peak_scores[..., None]), 0.0)
    totals = jnp.sum(weights, axis=-1)
    summed = jnp.einsum(
        "bvsgk,bkvd->bvsgd",
        weights.astype(jnp.bfloat16),
        value_rows,
        preferred_element_type=jnp.float32,
    )
    return (peak_scores, totals, summed)


def gather_by_exchange(piece, axis_name, count):
    spread = jnp.broadcast_to(piece[None], (count,) + piece.shape)
    return lax.all_to_all(spread, axis_name, split_axis=0, concat_axis=0, tiled=True)


def local(
    residual_input,
    input_norm_gain,
    query_weight,
    key_value_weight,
    output_weight,
    adapter_down_maps,
    adapter_query_up,
    adapter_key_value_up,
    adapter_output_down,
    adapter_output_up,
    request_adapter,
    prompt_length,
    cache_length,
    first_page_device,
    page_slot_table,
    cache_page_pool,
):
    holders = lax.axis_size("req")
    tensor_count = lax.axis_size("tensor")
    req_index = lax.axis_index("req")
    tensor_index = lax.axis_index("tensor")
    request_number = request_adapter.shape[0]
    cached_count = request_number // 2
    row_count = residual_input.shape[0]
    request_slot_rows = row_count // request_number
    piece_width = residual_input.shape[1]
    local_kv = key_value_weight.shape[1] // (2 * HEAD_SIZE)
    group_size = query_weight.shape[1] // (HEAD_SIZE * local_kv)
    page_rows = cache_page_pool.shape[1]
    tensor_count = lax.axis_size("tensor")
    gathered = lax.all_gather(residual_input, "tensor", axis=1, tiled=True)
    widened = gathered.astype(jnp.float32)
    inverse = lax.rsqrt(jnp.mean(widened * widened, axis=1, keepdims=True) + EPSILON)
    normed = (widened * inverse * input_norm_gain).astype(jnp.bfloat16)
    adapter_parts = (
        adapter_down_maps,
        adapter_query_up,
        adapter_key_value_up,
        adapter_output_down,
        adapter_output_up,
    )
    local_adapters = adapter_down_maps.shape[0]
    flat_parts = [part.reshape(local_adapters, -1) for part in adapter_parts]
    joined = jnp.concatenate(flat_parts, axis=1)
    lane_rows = joined.shape[1] // 128
    every_adapter = lax.all_gather(
        joined.reshape(local_adapters, lane_rows, 128), "req", axis=0, tiled=True
    )
    picked = jnp.take(every_adapter, request_adapter, axis=0, mode="clip").reshape(
        request_number, -1
    )
    picked_parts = []
    start = 0
    for part, flat in zip(adapter_parts, flat_parts):
        width = flat.shape[1]
        picked_parts.append(
            picked[:, start : start + width].reshape((request_number,) + part.shape[1:])
        )
        start += width
    down_picked, query_picked, key_value_picked, output_down_picked, oup_sel = picked_parts
    adapter_rank_size = query_picked.shape[1]
    own_columns = lax.dynamic_slice_in_dim(
        normed, tensor_index * piece_width, piece_width, 1
    ).reshape(request_number, request_slot_rows, piece_width)
    partial_low = jnp.einsum(
        "rsd,rkd->rsk", own_columns, down_picked, preferred_element_type=jnp.float32
    )
    reduced_input = (
        gather_by_exchange(partial_low.astype(jnp.bfloat16), "tensor", tensor_count)
        .astype(jnp.float32)
        .sum(axis=0)
        .astype(jnp.bfloat16)
    )
    query_rows = jnp.dot(normed, query_weight, preferred_element_type=jnp.float32).reshape(request_number, request_slot_rows, -1)
    query_rows = query_rows + ADAPTER_SCALE * jnp.einsum(
        "ibm,imf->ibf",
        reduced_input[..., :adapter_rank_size],
        query_picked,
        preferred_element_type=jnp.float32,
    )
    keyval = jnp.dot(normed, key_value_weight, preferred_element_type=jnp.float32).reshape(
        request_number, request_slot_rows, local_kv, 2 * HEAD_SIZE
    )
    key_add = jnp.einsum(
        "ibm,imf->ibf",
        reduced_input[..., adapter_rank_size : 2 * adapter_rank_size],
        key_value_picked[:, 0],
        preferred_element_type=jnp.float32,
    ).reshape(request_number, request_slot_rows, local_kv, HEAD_SIZE)
    value_add = jnp.einsum(
        "ibm,imf->ibf",
        reduced_input[..., 2 * adapter_rank_size :],
        key_value_picked[:, 1],
        preferred_element_type=jnp.float32,
    ).reshape(request_number, request_slot_rows, local_kv, HEAD_SIZE)
    my_cache = lax.dynamic_slice_in_dim(cache_length, req_index * cached_count, cached_count, 0)
    offsets = jnp.stack([jnp.zeros_like(my_cache), my_cache], axis=1).reshape(request_number)
    slot_index = jnp.arange(request_slot_rows, dtype=jnp.int32)
    positions = offsets[:, None] + slot_index[None, :]
    query_rot = rotate(
        query_rows.reshape(request_number, request_slot_rows, local_kv, group_size, HEAD_SIZE),
        positions[:, :, None, None],
    ).astype(jnp.bfloat16)
    key_rot = rotate(keyval[..., :HEAD_SIZE] + key_add, positions[:, :, None]).astype(jnp.bfloat16)
    value_new = (keyval[..., HEAD_SIZE:] + value_add).astype(jnp.bfloat16)
    causal = slot_index[None, :, None] >= slot_index[None, None, :]
    own_mask = causal & (slot_index[None, None, :] < prompt_length[:, None, None])
    own_part = partial_softmax(query_rot, key_rot, value_new, own_mask)
    asked_queries = query_rot[1::2]
    slot_order = page_slot_table[0].reshape(holders, cached_count).T.reshape(-1)
    outgoing = cache_page_pool[slot_order].reshape(
        cached_count, holders, page_rows, cache_page_pool.shape[2]
    )
    arrived = lax.all_to_all(outgoing, "req", split_axis=1, concat_axis=1, tiled=True)
    my_base = lax.dynamic_slice_in_dim(first_page_device, req_index * cached_count, cached_count, 0)
    page_of = (jnp.arange(holders, dtype=jnp.int32)[None, :] - my_base[:, None]) % holders
    key_pos = (
        page_of[:, :, None] * page_rows + jnp.arange(page_rows, dtype=jnp.int32)[None, None, :]
    ).reshape(cached_count, holders * page_rows)
    entries = arrived.reshape(cached_count, holders * page_rows, local_kv, 2 * HEAD_SIZE)
    visible = jnp.broadcast_to(
        (key_pos < my_cache[:, None])[:, None, :],
        (cached_count, request_slot_rows, holders * page_rows),
    )
    cache_part = partial_softmax(
        asked_queries, entries[..., :HEAD_SIZE], entries[..., HEAD_SIZE:], visible
    )
    filler = jnp.full_like(cache_part[0], NEG_FILL)
    spread_peak = jnp.stack([filler, cache_part[0]], axis=1).reshape(own_part[0].shape)
    spread_total = jnp.stack([jnp.zeros_like(cache_part[1]), cache_part[1]], axis=1).reshape(
        own_part[1].shape
    )
    spread_sum = jnp.stack([jnp.zeros_like(cache_part[2]), cache_part[2]], axis=1).reshape(
        own_part[2].shape
    )
    highest_all = jnp.maximum(own_part[0], spread_peak)
    own_weight = jnp.exp(own_part[0] - highest_all)
    cache_weight = jnp.exp(spread_peak - highest_all)
    denominator = own_part[1] * own_weight + spread_total * cache_weight
    numerator = own_part[2] * own_weight[..., None] + spread_sum * cache_weight[..., None]
    live_rows = slot_index[None, :] < prompt_length[:, None]
    attended = jnp.where(
        live_rows[:, None, :, None, None], numerator / denominator[..., None], 0.0
    ).astype(jnp.bfloat16)
    attended = jnp.transpose(attended, (0, 2, 1, 3, 4)).reshape(row_count, -1)
    head_terms = jnp.einsum(
        "sc,ctf->tsf",
        attended,
        output_weight.reshape(output_weight.shape[0], tensor_count, piece_width),
        preferred_element_type=jnp.float32,
    )
    low_part = jnp.einsum(
        "rsc,rkc->rsk",
        attended.reshape(request_number, request_slot_rows, -1),
        output_down_picked,
        preferred_element_type=jnp.float32,
    )
    reduced_output = (
        gather_by_exchange(low_part.astype(jnp.bfloat16), "tensor", tensor_count)
        .astype(jnp.float32)
        .sum(axis=0)
        .astype(jnp.bfloat16)
    )
    head_total = lax.psum_scatter(
        head_terms.astype(jnp.bfloat16), "tensor", scatter_dimension=0, tiled=False
    ).astype(jnp.float32)
    adapter_output = jnp.einsum(
        "ibm,imf->ibf", reduced_output, oup_sel, preferred_element_type=jnp.float32
    ).reshape(row_count, -1)
    return (head_total + ADAPTER_SCALE * adapter_output).astype(jnp.bfloat16)


def solution(mesh):
    placed = (
        P("req", "tensor"),
        P(),
        P(None, "tensor"),
        P(None, "tensor"),
        P("tensor", None),
        P("req", None, "tensor"),
        P("req", None, "tensor"),
        P("req", None, None, "tensor"),
        P("req", None, "tensor"),
        P("req", None, "tensor"),
        P("req"),
        P("req"),
        P(),
        P(),
        P("req", None),
        P("req", None, "tensor"),
    )
    return jax.shard_map(
        local, mesh=mesh, in_specs=placed, out_specs=P("req", "tensor"), check_vma=False
    )
```

```python
import jax
import jax.numpy as jnp
from jax import lax
from jax.sharding import PartitionSpec as P

HEAD_SIZE = 128


ROPE_BASE = 5000000.0
ADAPTER_SCALE = 2.0
EPSILON = 1e-05
NEG_FILL = -1e30


def rotate(vectors, positions):
    half_dim = vectors.shape[-1] // 2
    frequency = ROPE_BASE ** (-jnp.arange(half_dim, dtype=jnp.float32) / half_dim)
    angles = positions.astype(jnp.float32)[..., None] * frequency
    cosine = jnp.cos(angles)
    sine_part = jnp.sin(angles)
    front_half = vectors[..., :half_dim]
    back_half = vectors[..., half_dim:]
    return jnp.concatenate(
        [front_half * cosine - back_half * sine_part, back_half * cosine + front_half * sine_part],
        axis=-1,
    )


def partial_softmax(query_rows, key_rows, value_rows, allowed):
    score_scale = query_rows.shape[-1] ** (-0.5)
    scores = (
        jnp.einsum("bsvgd,bkvd->bvsgk", query_rows, key_rows, preferred_element_type=jnp.float32)
        * score_scale
    )
    spread_mask = allowed[:, None, :, None, :]
    scores = jnp.where(spread_mask, scores, NEG_FILL)
    peak_scores = jnp.max(scores, axis=-1)
    weights = jnp.where(spread_mask, jnp.exp(scores - peak_scores[..., None]), 0.0)
    totals = jnp.sum(weights, axis=-1)
    summed = jnp.einsum(
        "bvsgk,bkvd->bvsgd",
        weights.astype(jnp.bfloat16),
        value_rows,
        preferred_element_type=jnp.float32,
    )
    return (peak_scores, totals, summed)


def gather_by_exchange(piece, axis_name, count):
    spread = jnp.broadcast_to(piece[None], (count,) + piece.shape)
    return lax.all_to_all(spread, axis_name, split_axis=0, concat_axis=0, tiled=True)


def local(
    residual_input,
    input_norm_gain,
    query_weight,
    key_value_weight,
    output_weight,
    adapter_down_maps,
    adapter_query_up,
    adapter_key_value_up,
    adapter_output_down,
    adapter_output_up,
    request_adapter,
    prompt_length,
    cache_length,
    first_page_device,
    page_slot_table,
    cache_page_pool,
):
    holders = lax.axis_size("req")
    tensor_count = lax.axis_size("tensor")
    req_index = lax.axis_index("req")
    tensor_index = lax.axis_index("tensor")
    request_number = request_adapter.shape[0]
    cached_count = request_number // 2
    row_count = residual_input.shape[0]
    request_slot_rows = row_count // request_number
    piece_width = residual_input.shape[1]
    local_kv = key_value_weight.shape[1] // (2 * HEAD_SIZE)
    group_size = query_weight.shape[1] // (HEAD_SIZE * local_kv)
    page_rows = cache_page_pool.shape[1]
    tensor_count = lax.axis_size("tensor")
    gathered = lax.all_gather(residual_input, "tensor", axis=1, tiled=True)
    local_adapters = adapter_down_maps.shape[0]

    def pick_adapters(parts, by_exchange):
        flat_parts = [part.reshape(local_adapters, -1) for part in parts]
        joined = jnp.concatenate(flat_parts, axis=1)
        joined = joined.reshape(local_adapters, joined.shape[1] // 128, 128)
        if by_exchange:
            every_adapter = gather_by_exchange(joined, "req", holders).reshape(
                (holders * local_adapters,) + joined.shape[1:]
            )
        else:
            every_adapter = lax.all_gather(joined, "req", axis=0, tiled=True)
        picked = jnp.take(every_adapter, request_adapter, axis=0, mode="clip").reshape(
            request_number, -1
        )
        picked_parts = []
        start = 0
        for part, flat in zip(parts, flat_parts):
            width = flat.shape[1]
            picked_parts.append(
                picked[:, start : start + width].reshape((request_number,) + part.shape[1:])
            )
            start += width
        return picked_parts

    query_picked, key_value_picked, output_down_picked, oup_sel = pick_adapters(
        (adapter_query_up, adapter_key_value_up, adapter_output_down, adapter_output_up), True
    )
    gathered, held_down = lax.optimization_barrier((gathered, adapter_down_maps))
    (down_picked,) = pick_adapters((held_down,), False)
    widened = gathered.astype(jnp.float32)
    inverse = lax.rsqrt(jnp.mean(widened * widened, axis=1, keepdims=True) + EPSILON)
    normed = (widened * inverse * input_norm_gain).astype(jnp.bfloat16)
    adapter_rank_size = query_picked.shape[1]
    own_columns = lax.dynamic_slice_in_dim(
        normed, tensor_index * piece_width, piece_width, 1
    ).reshape(request_number, request_slot_rows, piece_width)
    partial_low = jnp.einsum(
        "rsd,rkd->rsk", own_columns, down_picked, preferred_element_type=jnp.float32
    )
    reduced_input = (
        gather_by_exchange(partial_low.astype(jnp.bfloat16), "tensor", tensor_count)
        .astype(jnp.float32)
        .sum(axis=0)
        .astype(jnp.bfloat16)
    )
    query_rows = jnp.dot(normed, query_weight, preferred_element_type=jnp.float32).reshape(request_number, request_slot_rows, -1)
    query_rows = query_rows + ADAPTER_SCALE * jnp.einsum(
        "ibm,imf->ibf",
        reduced_input[..., :adapter_rank_size],
        query_picked,
        preferred_element_type=jnp.float32,
    )
    keyval = jnp.dot(normed, key_value_weight, preferred_element_type=jnp.float32).reshape(
        request_number, request_slot_rows, local_kv, 2 * HEAD_SIZE
    )
    key_add = jnp.einsum(
        "ibm,imf->ibf",
        reduced_input[..., adapter_rank_size : 2 * adapter_rank_size],
        key_value_picked[:, 0],
        preferred_element_type=jnp.float32,
    ).reshape(request_number, request_slot_rows, local_kv, HEAD_SIZE)
    value_add = jnp.einsum(
        "ibm,imf->ibf",
        reduced_input[..., 2 * adapter_rank_size :],
        key_value_picked[:, 1],
        preferred_element_type=jnp.float32,
    ).reshape(request_number, request_slot_rows, local_kv, HEAD_SIZE)
    my_cache = lax.dynamic_slice_in_dim(cache_length, req_index * cached_count, cached_count, 0)
    offsets = jnp.stack([jnp.zeros_like(my_cache), my_cache], axis=1).reshape(request_number)
    slot_index = jnp.arange(request_slot_rows, dtype=jnp.int32)
    positions = offsets[:, None] + slot_index[None, :]
    query_rot = rotate(
        query_rows.reshape(request_number, request_slot_rows, local_kv, group_size, HEAD_SIZE),
        positions[:, :, None, None],
    ).astype(jnp.bfloat16)
    key_rot = rotate(keyval[..., :HEAD_SIZE] + key_add, positions[:, :, None]).astype(jnp.bfloat16)
    value_new = (keyval[..., HEAD_SIZE:] + value_add).astype(jnp.bfloat16)
    causal = slot_index[None, :, None] >= slot_index[None, None, :]
    own_mask = causal & (slot_index[None, None, :] < prompt_length[:, None, None])
    own_part = partial_softmax(query_rot, key_rot, value_new, own_mask)
    asked_queries = query_rot[1::2]
    slot_order = page_slot_table[0].reshape(holders, cached_count).T.reshape(-1)
    outgoing = cache_page_pool[slot_order].reshape(
        cached_count, holders, page_rows, cache_page_pool.shape[2]
    )
    arrived = lax.all_to_all(outgoing, "req", split_axis=1, concat_axis=1, tiled=True)
    my_base = lax.dynamic_slice_in_dim(first_page_device, req_index * cached_count, cached_count, 0)
    page_of = (jnp.arange(holders, dtype=jnp.int32)[None, :] - my_base[:, None]) % holders
    key_pos = (
        page_of[:, :, None] * page_rows + jnp.arange(page_rows, dtype=jnp.int32)[None, None, :]
    ).reshape(cached_count, holders * page_rows)
    entries = arrived.reshape(cached_count, holders * page_rows, local_kv, 2 * HEAD_SIZE)
    visible = jnp.broadcast_to(
        (key_pos < my_cache[:, None])[:, None, :],
        (cached_count, request_slot_rows, holders * page_rows),
    )
    cache_part = partial_softmax(
        asked_queries, entries[..., :HEAD_SIZE], entries[..., HEAD_SIZE:], visible
    )
    filler = jnp.full_like(cache_part[0], NEG_FILL)
    spread_peak = jnp.stack([filler, cache_part[0]], axis=1).reshape(own_part[0].shape)
    spread_total = jnp.stack([jnp.zeros_like(cache_part[1]), cache_part[1]], axis=1).reshape(
        own_part[1].shape
    )
    spread_sum = jnp.stack([jnp.zeros_like(cache_part[2]), cache_part[2]], axis=1).reshape(
        own_part[2].shape
    )
    highest_all = jnp.maximum(own_part[0], spread_peak)
    own_weight = jnp.exp(own_part[0] - highest_all)
    cache_weight = jnp.exp(spread_peak - highest_all)
    denominator = own_part[1] * own_weight + spread_total * cache_weight
    numerator = own_part[2] * own_weight[..., None] + spread_sum * cache_weight[..., None]
    live_rows = slot_index[None, :] < prompt_length[:, None]
    attended = jnp.where(
        live_rows[:, None, :, None, None], numerator / denominator[..., None], 0.0
    ).astype(jnp.bfloat16)
    attended = jnp.transpose(attended, (0, 2, 1, 3, 4)).reshape(row_count, -1)
    head_terms = jnp.einsum(
        "sc,ctf->tsf",
        attended,
        output_weight.reshape(output_weight.shape[0], tensor_count, piece_width),
        preferred_element_type=jnp.float32,
    )
    low_part = jnp.einsum(
        "rsc,rkc->rsk",
        attended.reshape(request_number, request_slot_rows, -1),
        output_down_picked,
        preferred_element_type=jnp.float32,
    )
    reduced_output = (
        gather_by_exchange(low_part.astype(jnp.bfloat16), "tensor", tensor_count)
        .astype(jnp.float32)
        .sum(axis=0)
        .astype(jnp.bfloat16)
    )
    head_total = lax.psum_scatter(
        head_terms.astype(jnp.bfloat16), "tensor", scatter_dimension=0, tiled=False
    ).astype(jnp.float32)
    adapter_output = jnp.einsum(
        "ibm,imf->ibf", reduced_output, oup_sel, preferred_element_type=jnp.float32
    ).reshape(row_count, -1)
    return (head_total + ADAPTER_SCALE * adapter_output).astype(jnp.bfloat16)


def solution(mesh):
    placed = (
        P("req", "tensor"),
        P(),
        P(None, "tensor"),
        P(None, "tensor"),
        P("tensor", None),
        P("req", None, "tensor"),
        P("req", None, "tensor"),
        P("req", None, None, "tensor"),
        P("req", None, "tensor"),
        P("req", None, "tensor"),
        P("req"),
        P("req"),
        P(),
        P(),
        P("req", None),
        P("req", None, "tensor"),
    )
    return jax.shard_map(
        local, mesh=mesh, in_specs=placed, out_specs=P("req", "tensor"), check_vma=False
    )
```

```python
import jax
import jax.numpy as jnp
from jax import lax
from jax.sharding import PartitionSpec as P

HEAD_SIZE = 128


ROPE_BASE = 5000000.0
ADAPTER_SCALE = 2.0
EPSILON = 1e-05
NEG_FILL = -1e30


def rotate(vectors, positions):
    half_dim = vectors.shape[-1] // 2
    frequency = ROPE_BASE ** (-jnp.arange(half_dim, dtype=jnp.float32) / half_dim)
    angles = positions.astype(jnp.float32)[..., None] * frequency
    cosine = jnp.cos(angles)
    sine_part = jnp.sin(angles)
    front_half = vectors[..., :half_dim]
    back_half = vectors[..., half_dim:]
    return jnp.concatenate(
        [front_half * cosine - back_half * sine_part, back_half * cosine + front_half * sine_part],
        axis=-1,
    )


def partial_softmax(query_rows, key_rows, value_rows, allowed):
    score_scale = query_rows.shape[-1] ** (-0.5)
    scores = (
        jnp.einsum("bsvgd,bkvd->bvsgk", query_rows, key_rows, preferred_element_type=jnp.float32)
        * score_scale
    )
    spread_mask = allowed[:, None, :, None, :]
    scores = jnp.where(spread_mask, scores, NEG_FILL)
    peak_scores = jnp.max(scores, axis=-1)
    weights = jnp.where(spread_mask, jnp.exp(scores - peak_scores[..., None]), 0.0)
    totals = jnp.sum(weights, axis=-1)
    summed = jnp.einsum(
        "bvsgk,bkvd->bvsgd",
        weights.astype(jnp.bfloat16),
        value_rows,
        preferred_element_type=jnp.float32,
    )
    return (peak_scores, totals, summed)


def gather_by_exchange(piece, axis_name, count):
    spread = jnp.broadcast_to(piece[None], (count,) + piece.shape)
    return lax.all_to_all(spread, axis_name, split_axis=0, concat_axis=0, tiled=True)


def local(
    residual_input,
    input_norm_gain,
    query_weight,
    key_value_weight,
    output_weight,
    adapter_down_maps,
    adapter_query_up,
    adapter_key_value_up,
    adapter_output_down,
    adapter_output_up,
    request_adapter,
    prompt_length,
    cache_length,
    first_page_device,
    page_slot_table,
    cache_page_pool,
):
    holders = lax.axis_size("req")
    tensor_count = lax.axis_size("tensor")
    req_index = lax.axis_index("req")
    tensor_index = lax.axis_index("tensor")
    request_number = request_adapter.shape[0]
    cached_count = request_number // 2
    row_count = residual_input.shape[0]
    request_slot_rows = row_count // request_number
    piece_width = residual_input.shape[1]
    local_kv = key_value_weight.shape[1] // (2 * HEAD_SIZE)
    group_size = query_weight.shape[1] // (HEAD_SIZE * local_kv)
    page_rows = cache_page_pool.shape[1]
    tensor_count = lax.axis_size("tensor")
    chip_count = tensor_count // 2
    core = tensor_index % 2
    chip = tensor_index // 2
    swap = [(index, index ^ 1) for index in range(tensor_count)]
    along = [
        (2 * ((target // 2 - 1) % chip_count), target)
        if target % 2 == 0
        else (2 * ((target // 2 + 1) % chip_count) + 1, target)
        for target in range(tensor_count)
    ]
    partner = lax.ppermute(residual_input, "tensor", swap)
    pair = jnp.where(
        core == 0,
        jnp.concatenate([residual_input, partner], axis=1),
        jnp.concatenate([partner, residual_input], axis=1),
    )
    beside = lax.ppermute(pair, "tensor", along)
    relayed = lax.ppermute(
        lax.dynamic_slice_in_dim(beside, core * piece_width, piece_width, 1), "tensor", along
    )
    held = jnp.concatenate([beside, relayed], axis=1)
    mirrored = lax.ppermute(held, "tensor", swap)
    pair_width = 2 * piece_width
    minus_piece = jnp.where(core == 0, held[:, :pair_width], mirrored[:, :pair_width])
    plus_piece = jnp.where(core == 0, mirrored[:, :pair_width], held[:, :pair_width])
    opposite = jnp.where(
        core == 0,
        jnp.concatenate([held[:, pair_width:], mirrored[:, pair_width:]], axis=1),
        jnp.concatenate([mirrored[:, pair_width:], held[:, pair_width:]], axis=1),
    )
    relative = jnp.stack([pair, plus_piece, opposite, minus_piece])
    chip_order = (jnp.arange(chip_count, dtype=jnp.int32) - chip) % chip_count
    gathered = jnp.take(relative, chip_order, axis=0)
    widened = gathered.astype(jnp.float32)
    inverse = lax.rsqrt(
        jnp.sum(widened * widened, axis=(0, 2), keepdims=True) / (tensor_count * piece_width)
        + EPSILON
    )
    normed_parts = (
        widened * inverse * input_norm_gain.reshape(chip_count, 1, pair_width)
    ).astype(jnp.bfloat16)
    own_normed = (
        residual_input.astype(jnp.float32)
        * inverse[0]
        * lax.dynamic_slice_in_dim(input_norm_gain, tensor_index * piece_width, piece_width, 0)
    ).astype(jnp.bfloat16)
    adapter_parts = (
        adapter_down_maps,
        adapter_query_up,
        adapter_key_value_up,
        adapter_output_down,
        adapter_output_up,
    )
    local_adapters = adapter_down_maps.shape[0]
    flat_parts = [part.reshape(local_adapters, -1) for part in adapter_parts]
    joined = jnp.concatenate(flat_parts, axis=1)
    lane_rows = joined.shape[1] // 128
    every_adapter = lax.all_gather(
        joined.reshape(local_adapters, lane_rows, 128), "req", axis=0, tiled=True
    )
    picked = jnp.take(every_adapter, request_adapter, axis=0, mode="clip").reshape(
        request_number, -1
    )
    picked_parts = []
    start = 0
    for part, flat in zip(adapter_parts, flat_parts):
        width = flat.shape[1]
        picked_parts.append(
            picked[:, start : start + width].reshape((request_number,) + part.shape[1:])
        )
        start += width
    down_picked, query_picked, key_value_picked, output_down_picked, oup_sel = picked_parts
    adapter_rank_size = query_picked.shape[1]
    own_columns = own_normed.reshape(request_number, request_slot_rows, piece_width)
    partial_low = jnp.einsum(
        "rsd,rkd->rsk", own_columns, down_picked, preferred_element_type=jnp.float32
    )
    reduced_input = (
        gather_by_exchange(partial_low.astype(jnp.bfloat16), "tensor", tensor_count)
        .astype(jnp.float32)
        .sum(axis=0)
        .astype(jnp.bfloat16)
    )
    query_rows = jnp.einsum(
        "csf,cfn->sn",
        normed_parts,
        query_weight.reshape(chip_count, pair_width, -1),
        preferred_element_type=jnp.float32,
    ).reshape(request_number, request_slot_rows, -1)
    query_rows = query_rows + ADAPTER_SCALE * jnp.einsum(
        "ibm,imf->ibf",
        reduced_input[..., :adapter_rank_size],
        query_picked,
        preferred_element_type=jnp.float32,
    )
    keyval = jnp.einsum(
        "csf,cfn->sn",
        normed_parts,
        key_value_weight.reshape(chip_count, pair_width, -1),
        preferred_element_type=jnp.float32,
    ).reshape(
        request_number, request_slot_rows, local_kv, 2 * HEAD_SIZE
    )
    key_add = jnp.einsum(
        "ibm,imf->ibf",
        reduced_input[..., adapter_rank_size : 2 * adapter_rank_size],
        key_value_picked[:, 0],
        preferred_element_type=jnp.float32,
    ).reshape(request_number, request_slot_rows, local_kv, HEAD_SIZE)
    value_add = jnp.einsum(
        "ibm,imf->ibf",
        reduced_input[..., 2 * adapter_rank_size :],
        key_value_picked[:, 1],
        preferred_element_type=jnp.float32,
    ).reshape(request_number, request_slot_rows, local_kv, HEAD_SIZE)
    my_cache = lax.dynamic_slice_in_dim(cache_length, req_index * cached_count, cached_count, 0)
    offsets = jnp.stack([jnp.zeros_like(my_cache), my_cache], axis=1).reshape(request_number)
    slot_index = jnp.arange(request_slot_rows, dtype=jnp.int32)
    positions = offsets[:, None] + slot_index[None, :]
    query_rot = rotate(
        query_rows.reshape(request_number, request_slot_rows, local_kv, group_size, HEAD_SIZE),
        positions[:, :, None, None],
    ).astype(jnp.bfloat16)
    key_rot = rotate(keyval[..., :HEAD_SIZE] + key_add, positions[:, :, None]).astype(jnp.bfloat16)
    value_new = (keyval[..., HEAD_SIZE:] + value_add).astype(jnp.bfloat16)
    causal = slot_index[None, :, None] >= slot_index[None, None, :]
    own_mask = causal & (slot_index[None, None, :] < prompt_length[:, None, None])
    own_part = partial_softmax(query_rot, key_rot, value_new, own_mask)
    asked_queries = query_rot[1::2]
    slot_order = page_slot_table[0].reshape(holders, cached_count).T.reshape(-1)
    outgoing = cache_page_pool[slot_order].reshape(
        cached_count, holders, page_rows, cache_page_pool.shape[2]
    )
    arrived = lax.all_to_all(outgoing, "req", split_axis=1, concat_axis=1, tiled=True)
    my_base = lax.dynamic_slice_in_dim(first_page_device, req_index * cached_count, cached_count, 0)
    page_of = (jnp.arange(holders, dtype=jnp.int32)[None, :] - my_base[:, None]) % holders
    key_pos = (
        page_of[:, :, None] * page_rows + jnp.arange(page_rows, dtype=jnp.int32)[None, None, :]
    ).reshape(cached_count, holders * page_rows)
    entries = arrived.reshape(cached_count, holders * page_rows, local_kv, 2 * HEAD_SIZE)
    visible = jnp.broadcast_to(
        (key_pos < my_cache[:, None])[:, None, :],
        (cached_count, request_slot_rows, holders * page_rows),
    )
    cache_part = partial_softmax(
        asked_queries, entries[..., :HEAD_SIZE], entries[..., HEAD_SIZE:], visible
    )
    filler = jnp.full_like(cache_part[0], NEG_FILL)
    spread_peak = jnp.stack([filler, cache_part[0]], axis=1).reshape(own_part[0].shape)
    spread_total = jnp.stack([jnp.zeros_like(cache_part[1]), cache_part[1]], axis=1).reshape(
        own_part[1].shape
    )
    spread_sum = jnp.stack([jnp.zeros_like(cache_part[2]), cache_part[2]], axis=1).reshape(
        own_part[2].shape
    )
    highest_all = jnp.maximum(own_part[0], spread_peak)
    own_weight = jnp.exp(own_part[0] - highest_all)
    cache_weight = jnp.exp(spread_peak - highest_all)
    denominator = own_part[1] * own_weight + spread_total * cache_weight
    numerator = own_part[2] * own_weight[..., None] + spread_sum * cache_weight[..., None]
    live_rows = slot_index[None, :] < prompt_length[:, None]
    attended = jnp.where(
        live_rows[:, None, :, None, None], numerator / denominator[..., None], 0.0
    ).astype(jnp.bfloat16)
    attended = jnp.transpose(attended, (0, 2, 1, 3, 4)).reshape(row_count, -1)
    head_terms = jnp.einsum(
        "sc,ctf->tsf",
        attended,
        output_weight.reshape(output_weight.shape[0], tensor_count, piece_width),
        preferred_element_type=jnp.float32,
    )
    low_part = jnp.einsum(
        "rsc,rkc->rsk",
        attended.reshape(request_number, request_slot_rows, -1),
        output_down_picked,
        preferred_element_type=jnp.float32,
    )
    reduced_output = (
        gather_by_exchange(low_part.astype(jnp.bfloat16), "tensor", tensor_count)
        .astype(jnp.float32)
        .sum(axis=0)
        .astype(jnp.bfloat16)
    )
    head_total = lax.psum_scatter(
        head_terms.astype(jnp.bfloat16), "tensor", scatter_dimension=0, tiled=False
    ).astype(jnp.float32)
    adapter_output = jnp.einsum(
        "ibm,imf->ibf", reduced_output, oup_sel, preferred_element_type=jnp.float32
    ).reshape(row_count, -1)
    return (head_total + ADAPTER_SCALE * adapter_output).astype(jnp.bfloat16)


def solution(mesh):
    placed = (
        P("req", "tensor"),
        P(),
        P(None, "tensor"),
        P(None, "tensor"),
        P("tensor", None),
        P("req", None, "tensor"),
        P("req", None, "tensor"),
        P("req", None, None, "tensor"),
        P("req", None, "tensor"),
        P("req", None, "tensor"),
        P("req"),
        P("req"),
        P(),
        P(),
        P("req", None),
        P("req", None, "tensor"),
    )
    return jax.shard_map(
        local, mesh=mesh, in_specs=placed, out_specs=P("req", "tensor"), check_vma=False
    )
```

```python
import jax
import jax.numpy as jnp
from jax import lax
from jax.sharding import PartitionSpec as P

HEAD_SIZE = 128


ROPE_BASE = 5000000.0
ADAPTER_SCALE = 2.0
EPSILON = 1e-05
NEG_FILL = -1e30


def rotate(vectors, positions):
    half_dim = vectors.shape[-1] // 2
    frequency = ROPE_BASE ** (-jnp.arange(half_dim, dtype=jnp.float32) / half_dim)
    angles = positions.astype(jnp.float32)[..., None] * frequency
    cosine = jnp.cos(angles)
    sine_part = jnp.sin(angles)
    front_half = vectors[..., :half_dim]
    back_half = vectors[..., half_dim:]
    return jnp.concatenate(
        [front_half * cosine - back_half * sine_part, back_half * cosine + front_half * sine_part],
        axis=-1,
    )


def partial_softmax(query_rows, key_rows, value_rows, allowed):
    score_scale = query_rows.shape[-1] ** (-0.5)
    scores = (
        jnp.einsum("bsvgd,bkvd->bvsgk", query_rows, key_rows, preferred_element_type=jnp.float32)
        * score_scale
    )
    spread_mask = allowed[:, None, :, None, :]
    scores = jnp.where(spread_mask, scores, NEG_FILL)
    peak_scores = jnp.max(scores, axis=-1)
    weights = jnp.where(spread_mask, jnp.exp(scores - peak_scores[..., None]), 0.0)
    totals = jnp.sum(weights, axis=-1)
    summed = jnp.einsum(
        "bvsgk,bkvd->bvsgd",
        weights.astype(jnp.bfloat16),
        value_rows,
        preferred_element_type=jnp.float32,
    )
    return (peak_scores, totals, summed)


def gather_by_exchange(piece, axis_name, count):
    spread = jnp.broadcast_to(piece[None], (count,) + piece.shape)
    return lax.all_to_all(spread, axis_name, split_axis=0, concat_axis=0, tiled=True)


def local(
    residual_input,
    input_norm_gain,
    query_weight,
    key_value_weight,
    output_weight,
    adapter_down_maps,
    adapter_query_up,
    adapter_key_value_up,
    adapter_output_down,
    adapter_output_up,
    request_adapter,
    prompt_length,
    cache_length,
    first_page_device,
    page_slot_table,
    cache_page_pool,
):
    holders = lax.axis_size("req")
    tensor_count = lax.axis_size("tensor")
    req_index = lax.axis_index("req")
    tensor_index = lax.axis_index("tensor")
    request_number = request_adapter.shape[0]
    cached_count = request_number // 2
    row_count = residual_input.shape[0]
    request_slot_rows = row_count // request_number
    piece_width = residual_input.shape[1]
    local_kv = key_value_weight.shape[1] // (2 * HEAD_SIZE)
    group_size = query_weight.shape[1] // (HEAD_SIZE * local_kv)
    page_rows = cache_page_pool.shape[1]
    tensor_count = lax.axis_size("tensor")
    chip_count = tensor_count // 2
    core = tensor_index % 2
    chip = tensor_index // 2
    swap = [(index, index ^ 1) for index in range(tensor_count)]
    along = [
        (2 * ((target // 2 - 1) % chip_count), target)
        if target % 2 == 0
        else (2 * ((target // 2 + 1) % chip_count) + 1, target)
        for target in range(tensor_count)
    ]
    partner = lax.ppermute(residual_input, "tensor", swap)
    pair = jnp.where(
        core == 0,
        jnp.concatenate([residual_input, partner], axis=1),
        jnp.concatenate([partner, residual_input], axis=1),
    )
    beside = lax.ppermute(pair, "tensor", along)
    relayed = lax.ppermute(
        lax.dynamic_slice_in_dim(beside, core * piece_width, piece_width, 1), "tensor", along
    )
    held = jnp.concatenate([beside, relayed], axis=1)
    mirrored = lax.ppermute(held, "tensor", swap)
    pair_width = 2 * piece_width
    minus_piece = jnp.where(core == 0, held[:, :pair_width], mirrored[:, :pair_width])
    plus_piece = jnp.where(core == 0, mirrored[:, :pair_width], held[:, :pair_width])
    opposite = jnp.where(
        core == 0,
        jnp.concatenate([held[:, pair_width:], mirrored[:, pair_width:]], axis=1),
        jnp.concatenate([mirrored[:, pair_width:], held[:, pair_width:]], axis=1),
    )
    relative = jnp.stack([pair, plus_piece, opposite, minus_piece])
    chip_order = (jnp.arange(chip_count, dtype=jnp.int32) - chip) % chip_count
    gathered = jnp.take(relative, chip_order, axis=0)
    widened = gathered.astype(jnp.float32)
    inverse = lax.rsqrt(
        jnp.sum(widened * widened, axis=(0, 2), keepdims=True) / (tensor_count * piece_width)
        + EPSILON
    )
    normed_parts = (
        widened * inverse * input_norm_gain.reshape(chip_count, 1, pair_width)
    ).astype(jnp.bfloat16)
    own_normed = (
        residual_input.astype(jnp.float32)
        * inverse[0]
        * lax.dynamic_slice_in_dim(input_norm_gain, tensor_index * piece_width, piece_width, 0)
    ).astype(jnp.bfloat16)
    adapter_parts = (
        adapter_down_maps,
        adapter_query_up,
        adapter_key_value_up,
        adapter_output_down,
        adapter_output_up,
    )
    local_adapters = adapter_down_maps.shape[0]
    flat_parts = [part.reshape(local_adapters, -1) for part in adapter_parts]
    joined = jnp.concatenate(flat_parts, axis=1)
    lane_rows = joined.shape[1] // 128
    every_adapter = lax.all_gather(
        joined.reshape(local_adapters, lane_rows, 128), "req", axis=0, tiled=True
    )
    every_adapter, cache_page_pool = lax.optimization_barrier((every_adapter, cache_page_pool))
    picked = jnp.take(every_adapter, request_adapter, axis=0, mode="clip").reshape(
        request_number, -1
    )
    picked_parts = []
    start = 0
    for part, flat in zip(adapter_parts, flat_parts):
        width = flat.shape[1]
        picked_parts.append(
            picked[:, start : start + width].reshape((request_number,) + part.shape[1:])
        )
        start += width
    down_picked, query_picked, key_value_picked, output_down_picked, oup_sel = picked_parts
    adapter_rank_size = query_picked.shape[1]
    own_columns = own_normed.reshape(request_number, request_slot_rows, piece_width)
    partial_low = jnp.einsum(
        "rsd,rkd->rsk", own_columns, down_picked, preferred_element_type=jnp.float32
    )
    reduced_input = (
        gather_by_exchange(partial_low.astype(jnp.bfloat16), "tensor", tensor_count)
        .astype(jnp.float32)
        .sum(axis=0)
        .astype(jnp.bfloat16)
    )
    query_rows = jnp.einsum(
        "csf,cfn->sn",
        normed_parts,
        query_weight.reshape(chip_count, pair_width, -1),
        preferred_element_type=jnp.float32,
    ).reshape(request_number, request_slot_rows, -1)
    query_rows = query_rows + ADAPTER_SCALE * jnp.einsum(
        "ibm,imf->ibf",
        reduced_input[..., :adapter_rank_size],
        query_picked,
        preferred_element_type=jnp.float32,
    )
    keyval = jnp.einsum(
        "csf,cfn->sn",
        normed_parts,
        key_value_weight.reshape(chip_count, pair_width, -1),
        preferred_element_type=jnp.float32,
    ).reshape(
        request_number, request_slot_rows, local_kv, 2 * HEAD_SIZE
    )
    key_add = jnp.einsum(
        "ibm,imf->ibf",
        reduced_input[..., adapter_rank_size : 2 * adapter_rank_size],
        key_value_picked[:, 0],
        preferred_element_type=jnp.float32,
    ).reshape(request_number, request_slot_rows, local_kv, HEAD_SIZE)
    value_add = jnp.einsum(
        "ibm,imf->ibf",
        reduced_input[..., 2 * adapter_rank_size :],
        key_value_picked[:, 1],
        preferred_element_type=jnp.float32,
    ).reshape(request_number, request_slot_rows, local_kv, HEAD_SIZE)
    my_cache = lax.dynamic_slice_in_dim(cache_length, req_index * cached_count, cached_count, 0)
    offsets = jnp.stack([jnp.zeros_like(my_cache), my_cache], axis=1).reshape(request_number)
    slot_index = jnp.arange(request_slot_rows, dtype=jnp.int32)
    positions = offsets[:, None] + slot_index[None, :]
    query_rot = rotate(
        query_rows.reshape(request_number, request_slot_rows, local_kv, group_size, HEAD_SIZE),
        positions[:, :, None, None],
    ).astype(jnp.bfloat16)
    key_rot = rotate(keyval[..., :HEAD_SIZE] + key_add, positions[:, :, None]).astype(jnp.bfloat16)
    value_new = (keyval[..., HEAD_SIZE:] + value_add).astype(jnp.bfloat16)
    causal = slot_index[None, :, None] >= slot_index[None, None, :]
    own_mask = causal & (slot_index[None, None, :] < prompt_length[:, None, None])
    own_part = partial_softmax(query_rot, key_rot, value_new, own_mask)
    asked_queries = query_rot[1::2]
    slot_order = page_slot_table[0].reshape(holders, cached_count).T.reshape(-1)
    outgoing = cache_page_pool[slot_order].reshape(
        cached_count, holders, page_rows, cache_page_pool.shape[2]
    )
    arrived = lax.all_to_all(outgoing, "req", split_axis=1, concat_axis=1, tiled=True)
    my_base = lax.dynamic_slice_in_dim(first_page_device, req_index * cached_count, cached_count, 0)
    page_of = (jnp.arange(holders, dtype=jnp.int32)[None, :] - my_base[:, None]) % holders
    key_pos = (
        page_of[:, :, None] * page_rows + jnp.arange(page_rows, dtype=jnp.int32)[None, None, :]
    ).reshape(cached_count, holders * page_rows)
    entries = arrived.reshape(cached_count, holders * page_rows, local_kv, 2 * HEAD_SIZE)
    visible = jnp.broadcast_to(
        (key_pos < my_cache[:, None])[:, None, :],
        (cached_count, request_slot_rows, holders * page_rows),
    )
    cache_part = partial_softmax(
        asked_queries, entries[..., :HEAD_SIZE], entries[..., HEAD_SIZE:], visible
    )
    filler = jnp.full_like(cache_part[0], NEG_FILL)
    spread_peak = jnp.stack([filler, cache_part[0]], axis=1).reshape(own_part[0].shape)
    spread_total = jnp.stack([jnp.zeros_like(cache_part[1]), cache_part[1]], axis=1).reshape(
        own_part[1].shape
    )
    spread_sum = jnp.stack([jnp.zeros_like(cache_part[2]), cache_part[2]], axis=1).reshape(
        own_part[2].shape
    )
    highest_all = jnp.maximum(own_part[0], spread_peak)
    own_weight = jnp.exp(own_part[0] - highest_all)
    cache_weight = jnp.exp(spread_peak - highest_all)
    denominator = own_part[1] * own_weight + spread_total * cache_weight
    numerator = own_part[2] * own_weight[..., None] + spread_sum * cache_weight[..., None]
    live_rows = slot_index[None, :] < prompt_length[:, None]
    attended = jnp.where(
        live_rows[:, None, :, None, None], numerator / denominator[..., None], 0.0
    ).astype(jnp.bfloat16)
    attended = jnp.transpose(attended, (0, 2, 1, 3, 4)).reshape(row_count, -1)
    head_terms = jnp.einsum(
        "sc,ctf->tsf",
        attended,
        output_weight.reshape(output_weight.shape[0], tensor_count, piece_width),
        preferred_element_type=jnp.float32,
    )
    low_part = jnp.einsum(
        "rsc,rkc->rsk",
        attended.reshape(request_number, request_slot_rows, -1),
        output_down_picked,
        preferred_element_type=jnp.float32,
    )
    reduced_output = (
        gather_by_exchange(low_part.astype(jnp.bfloat16), "tensor", tensor_count)
        .astype(jnp.float32)
        .sum(axis=0)
        .astype(jnp.bfloat16)
    )
    head_total = lax.psum_scatter(
        head_terms.astype(jnp.bfloat16), "tensor", scatter_dimension=0, tiled=False
    ).astype(jnp.float32)
    adapter_output = jnp.einsum(
        "ibm,imf->ibf", reduced_output, oup_sel, preferred_element_type=jnp.float32
    ).reshape(row_count, -1)
    return (head_total + ADAPTER_SCALE * adapter_output).astype(jnp.bfloat16)


def solution(mesh):
    placed = (
        P("req", "tensor"),
        P(),
        P(None, "tensor"),
        P(None, "tensor"),
        P("tensor", None),
        P("req", None, "tensor"),
        P("req", None, "tensor"),
        P("req", None, None, "tensor"),
        P("req", None, "tensor"),
        P("req", None, "tensor"),
        P("req"),
        P("req"),
        P(),
        P(),
        P("req", None),
        P("req", None, "tensor"),
    )
    return jax.shard_map(
        local, mesh=mesh, in_specs=placed, out_specs=P("req", "tensor"), check_vma=False
    )
```

```python
import jax
import jax.numpy as jnp
from jax import lax
from jax.sharding import PartitionSpec as P

HEAD_SIZE = 128


ROPE_BASE = 5000000.0
ADAPTER_SCALE = 2.0
EPSILON = 1e-05
NEG_FILL = -1e30


def rotate(vectors, positions):
    half_dim = vectors.shape[-1] // 2
    frequency = ROPE_BASE ** (-jnp.arange(half_dim, dtype=jnp.float32) / half_dim)
    angles = positions.astype(jnp.float32)[..., None] * frequency
    cosine = jnp.cos(angles)
    sine_part = jnp.sin(angles)
    front_half = vectors[..., :half_dim]
    back_half = vectors[..., half_dim:]
    return jnp.concatenate(
        [front_half * cosine - back_half * sine_part, back_half * cosine + front_half * sine_part],
        axis=-1,
    )


def partial_softmax(query_rows, key_rows, value_rows, allowed):
    score_scale = query_rows.shape[-1] ** (-0.5)
    scores = (
        jnp.einsum("bsvgd,bkvd->bvsgk", query_rows, key_rows, preferred_element_type=jnp.float32)
        * score_scale
    )
    spread_mask = allowed[:, None, :, None, :]
    scores = jnp.where(spread_mask, scores, NEG_FILL)
    peak_scores = jnp.max(scores, axis=-1)
    weights = jnp.where(spread_mask, jnp.exp(scores - peak_scores[..., None]), 0.0)
    totals = jnp.sum(weights, axis=-1)
    summed = jnp.einsum(
        "bvsgk,bkvd->bvsgd",
        weights.astype(jnp.bfloat16),
        value_rows,
        preferred_element_type=jnp.float32,
    )
    return (peak_scores, totals, summed)


def gather_by_exchange(piece, axis_name, count):
    spread = jnp.broadcast_to(piece[None], (count,) + piece.shape)
    return lax.all_to_all(spread, axis_name, split_axis=0, concat_axis=0, tiled=True)


def sum_over_tensor(partial, count):
    total = partial.astype(jnp.bfloat16).astype(jnp.float32)
    step = 1
    while step < count:
        pairs = [(index, index ^ step) for index in range(count)]
        sent = total.astype(jnp.bfloat16)
        total = sent.astype(jnp.float32) + lax.ppermute(sent, "tensor", pairs).astype(jnp.float32)
        step *= 2
    return total


def local(
    residual_input,
    input_norm_gain,
    query_weight,
    key_value_weight,
    output_weight,
    adapter_down_maps,
    adapter_query_up,
    adapter_key_value_up,
    adapter_output_down,
    adapter_output_up,
    request_adapter,
    prompt_length,
    cache_length,
    first_page_device,
    page_slot_table,
    cache_page_pool,
):
    holders = lax.axis_size("req")
    tensor_count = lax.axis_size("tensor")
    req_index = lax.axis_index("req")
    tensor_index = lax.axis_index("tensor")
    request_number = request_adapter.shape[0]
    cached_count = request_number // 2
    row_count = residual_input.shape[0]
    request_slot_rows = row_count // request_number
    piece_width = residual_input.shape[1]
    local_kv = key_value_weight.shape[1] // (2 * HEAD_SIZE)
    group_size = query_weight.shape[1] // (HEAD_SIZE * local_kv)
    page_rows = cache_page_pool.shape[1]
    tensor_count = lax.axis_size("tensor")
    chip_count = tensor_count // 2
    core = tensor_index % 2
    chip = tensor_index // 2
    swap = [(index, index ^ 1) for index in range(tensor_count)]
    along = [
        (2 * ((target // 2 - 1) % chip_count), target)
        if target % 2 == 0
        else (2 * ((target // 2 + 1) % chip_count) + 1, target)
        for target in range(tensor_count)
    ]
    partner = lax.ppermute(residual_input, "tensor", swap)
    pair = jnp.where(
        core == 0,
        jnp.concatenate([residual_input, partner], axis=1),
        jnp.concatenate([partner, residual_input], axis=1),
    )
    beside = lax.ppermute(pair, "tensor", along)
    relayed = lax.ppermute(
        lax.dynamic_slice_in_dim(beside, core * piece_width, piece_width, 1), "tensor", along
    )
    held = jnp.concatenate([beside, relayed], axis=1)
    mirrored = lax.ppermute(held, "tensor", swap)
    pair_width = 2 * piece_width
    minus_piece = jnp.where(core == 0, held[:, :pair_width], mirrored[:, :pair_width])
    plus_piece = jnp.where(core == 0, mirrored[:, :pair_width], held[:, :pair_width])
    opposite = jnp.where(
        core == 0,
        jnp.concatenate([held[:, pair_width:], mirrored[:, pair_width:]], axis=1),
        jnp.concatenate([mirrored[:, pair_width:], held[:, pair_width:]], axis=1),
    )
    relative = jnp.stack([pair, plus_piece, opposite, minus_piece])
    chip_order = (jnp.arange(chip_count, dtype=jnp.int32) - chip) % chip_count
    gathered = jnp.take(relative, chip_order, axis=0)
    widened = gathered.astype(jnp.float32)
    inverse = lax.rsqrt(
        jnp.sum(widened * widened, axis=(0, 2), keepdims=True) / (tensor_count * piece_width)
        + EPSILON
    )
    normed_parts = (
        widened * inverse * input_norm_gain.reshape(chip_count, 1, pair_width)
    ).astype(jnp.bfloat16)
    own_normed = (
        residual_input.astype(jnp.float32)
        * inverse[0]
        * lax.dynamic_slice_in_dim(input_norm_gain, tensor_index * piece_width, piece_width, 0)
    ).astype(jnp.bfloat16)
    adapter_parts = (
        adapter_down_maps,
        adapter_query_up,
        adapter_key_value_up,
        adapter_output_down,
        adapter_output_up,
    )
    local_adapters = adapter_down_maps.shape[0]
    flat_parts = [part.reshape(local_adapters, -1) for part in adapter_parts]
    joined = jnp.concatenate(flat_parts, axis=1)
    lane_rows = joined.shape[1] // 128
    every_adapter = lax.all_gather(
        joined.reshape(local_adapters, lane_rows, 128), "req", axis=0, tiled=True
    )
    slot_order = page_slot_table[0].reshape(holders, cached_count).T.reshape(-1)
    outgoing = cache_page_pool[slot_order].reshape(
        cached_count, holders, page_rows, cache_page_pool.shape[2]
    )
    every_adapter, outgoing = lax.optimization_barrier((every_adapter, outgoing))
    arrived = lax.all_to_all(outgoing, "req", split_axis=1, concat_axis=1, tiled=True)
    picked = jnp.take(every_adapter, request_adapter, axis=0, mode="clip").reshape(
        request_number, -1
    )
    picked_parts = []
    start = 0
    for part, flat in zip(adapter_parts, flat_parts):
        width = flat.shape[1]
        picked_parts.append(
            picked[:, start : start + width].reshape((request_number,) + part.shape[1:])
        )
        start += width
    down_picked, query_picked, key_value_picked, output_down_picked, oup_sel = picked_parts
    adapter_rank_size = query_picked.shape[1]
    own_columns = own_normed.reshape(request_number, request_slot_rows, piece_width)
    partial_low = jnp.einsum(
        "rsd,rkd->rsk", own_columns, down_picked, preferred_element_type=jnp.float32
    )
    reduced_input = sum_over_tensor(partial_low, tensor_count).astype(jnp.bfloat16)
    query_rows = jnp.einsum(
        "csf,cfn->sn",
        normed_parts,
        query_weight.reshape(chip_count, pair_width, -1),
        preferred_element_type=jnp.float32,
    ).reshape(request_number, request_slot_rows, -1)
    query_rows = query_rows + ADAPTER_SCALE * jnp.einsum(
        "ibm,imf->ibf",
        reduced_input[..., :adapter_rank_size],
        query_picked,
        preferred_element_type=jnp.float32,
    )
    keyval = jnp.einsum(
        "csf,cfn->sn",
        normed_parts,
        key_value_weight.reshape(chip_count, pair_width, -1),
        preferred_element_type=jnp.float32,
    ).reshape(
        request_number, request_slot_rows, local_kv, 2 * HEAD_SIZE
    )
    key_add = jnp.einsum(
        "ibm,imf->ibf",
        reduced_input[..., adapter_rank_size : 2 * adapter_rank_size],
        key_value_picked[:, 0],
        preferred_element_type=jnp.float32,
    ).reshape(request_number, request_slot_rows, local_kv, HEAD_SIZE)
    value_add = jnp.einsum(
        "ibm,imf->ibf",
        reduced_input[..., 2 * adapter_rank_size :],
        key_value_picked[:, 1],
        preferred_element_type=jnp.float32,
    ).reshape(request_number, request_slot_rows, local_kv, HEAD_SIZE)
    my_cache = lax.dynamic_slice_in_dim(cache_length, req_index * cached_count, cached_count, 0)
    offsets = jnp.stack([jnp.zeros_like(my_cache), my_cache], axis=1).reshape(request_number)
    slot_index = jnp.arange(request_slot_rows, dtype=jnp.int32)
    positions = offsets[:, None] + slot_index[None, :]
    query_rot = rotate(
        query_rows.reshape(request_number, request_slot_rows, local_kv, group_size, HEAD_SIZE),
        positions[:, :, None, None],
    ).astype(jnp.bfloat16)
    key_rot = rotate(keyval[..., :HEAD_SIZE] + key_add, positions[:, :, None]).astype(jnp.bfloat16)
    value_new = (keyval[..., HEAD_SIZE:] + value_add).astype(jnp.bfloat16)
    causal = slot_index[None, :, None] >= slot_index[None, None, :]
    own_mask = causal & (slot_index[None, None, :] < prompt_length[:, None, None])
    own_part = partial_softmax(query_rot, key_rot, value_new, own_mask)
    asked_queries = query_rot[1::2]
    my_base = lax.dynamic_slice_in_dim(first_page_device, req_index * cached_count, cached_count, 0)
    page_of = (jnp.arange(holders, dtype=jnp.int32)[None, :] - my_base[:, None]) % holders
    key_pos = (
        page_of[:, :, None] * page_rows + jnp.arange(page_rows, dtype=jnp.int32)[None, None, :]
    ).reshape(cached_count, holders * page_rows)
    entries = arrived.reshape(cached_count, holders * page_rows, local_kv, 2 * HEAD_SIZE)
    visible = jnp.broadcast_to(
        (key_pos < my_cache[:, None])[:, None, :],
        (cached_count, request_slot_rows, holders * page_rows),
    )
    cache_part = partial_softmax(
        asked_queries, entries[..., :HEAD_SIZE], entries[..., HEAD_SIZE:], visible
    )
    filler = jnp.full_like(cache_part[0], NEG_FILL)
    spread_peak = jnp.stack([filler, cache_part[0]], axis=1).reshape(own_part[0].shape)
    spread_total = jnp.stack([jnp.zeros_like(cache_part[1]), cache_part[1]], axis=1).reshape(
        own_part[1].shape
    )
    spread_sum = jnp.stack([jnp.zeros_like(cache_part[2]), cache_part[2]], axis=1).reshape(
        own_part[2].shape
    )
    highest_all = jnp.maximum(own_part[0], spread_peak)
    own_weight = jnp.exp(own_part[0] - highest_all)
    cache_weight = jnp.exp(spread_peak - highest_all)
    denominator = own_part[1] * own_weight + spread_total * cache_weight
    numerator = own_part[2] * own_weight[..., None] + spread_sum * cache_weight[..., None]
    live_rows = slot_index[None, :] < prompt_length[:, None]
    attended = jnp.where(
        live_rows[:, None, :, None, None], numerator / denominator[..., None], 0.0
    ).astype(jnp.bfloat16)
    attended = jnp.transpose(attended, (0, 2, 1, 3, 4)).reshape(row_count, -1)
    head_terms = jnp.einsum(
        "sc,ctf->tsf",
        attended,
        output_weight.reshape(output_weight.shape[0], tensor_count, piece_width),
        preferred_element_type=jnp.float32,
    )
    low_part = jnp.einsum(
        "rsc,rkc->rsk",
        attended.reshape(request_number, request_slot_rows, -1),
        output_down_picked,
        preferred_element_type=jnp.float32,
    )
    reduced_output = sum_over_tensor(low_part, tensor_count).astype(jnp.bfloat16)
    head_total = lax.psum_scatter(
        head_terms.astype(jnp.bfloat16), "tensor", scatter_dimension=0, tiled=False
    ).astype(jnp.float32)
    adapter_output = jnp.einsum(
        "ibm,imf->ibf", reduced_output, oup_sel, preferred_element_type=jnp.float32
    ).reshape(row_count, -1)
    return (head_total + ADAPTER_SCALE * adapter_output).astype(jnp.bfloat16)


def solution(mesh):
    placed = (
        P("req", "tensor"),
        P(),
        P(None, "tensor"),
        P(None, "tensor"),
        P("tensor", None),
        P("req", None, "tensor"),
        P("req", None, "tensor"),
        P("req", None, None, "tensor"),
        P("req", None, "tensor"),
        P("req", None, "tensor"),
        P("req"),
        P("req"),
        P(),
        P(),
        P("req", None),
        P("req", None, "tensor"),
    )
    return jax.shard_map(
        local, mesh=mesh, in_specs=placed, out_specs=P("req", "tensor"), check_vma=False
    )
```

```python
import jax
import jax.numpy as jnp
from jax import lax
from jax.sharding import PartitionSpec as P

HEAD_SIZE = 128


ROPE_BASE = 5000000.0
ADAPTER_SCALE = 2.0
EPSILON = 1e-05
NEG_FILL = -1e30


def rotate(vectors, positions):
    half_dim = vectors.shape[-1] // 2
    frequency = ROPE_BASE ** (-jnp.arange(half_dim, dtype=jnp.float32) / half_dim)
    angles = positions.astype(jnp.float32)[..., None] * frequency
    cosine = jnp.cos(angles)
    sine_part = jnp.sin(angles)
    front_half = vectors[..., :half_dim]
    back_half = vectors[..., half_dim:]
    return jnp.concatenate(
        [front_half * cosine - back_half * sine_part, back_half * cosine + front_half * sine_part],
        axis=-1,
    )


def partial_softmax(query_rows, key_rows, value_rows, allowed):
    score_scale = query_rows.shape[-1] ** (-0.5)
    scores = (
        jnp.einsum("bsvgd,bkvd->bvsgk", query_rows, key_rows, preferred_element_type=jnp.float32)
        * score_scale
    )
    spread_mask = allowed[:, None, :, None, :]
    scores = jnp.where(spread_mask, scores, NEG_FILL)
    peak_scores = jnp.max(scores, axis=-1)
    weights = jnp.where(spread_mask, jnp.exp(scores - peak_scores[..., None]), 0.0)
    totals = jnp.sum(weights, axis=-1)
    summed = jnp.einsum(
        "bvsgk,bkvd->bvsgd",
        weights.astype(jnp.bfloat16),
        value_rows,
        preferred_element_type=jnp.float32,
    )
    return (peak_scores, totals, summed)


def gather_by_exchange(piece, axis_name, count):
    spread = jnp.broadcast_to(piece[None], (count,) + piece.shape)
    return lax.all_to_all(spread, axis_name, split_axis=0, concat_axis=0, tiled=True)


def sum_over_tensor(partial, count):
    total = partial.astype(jnp.bfloat16).astype(jnp.float32)
    step = 1
    while step < count:
        pairs = [(index, index ^ step) for index in range(count)]
        sent = total.astype(jnp.bfloat16)
        total = sent.astype(jnp.float32) + lax.ppermute(sent, "tensor", pairs).astype(jnp.float32)
        step *= 2
    return total


def local(
    residual_input,
    input_norm_gain,
    query_weight,
    key_value_weight,
    output_weight,
    adapter_down_maps,
    adapter_query_up,
    adapter_key_value_up,
    adapter_output_down,
    adapter_output_up,
    request_adapter,
    prompt_length,
    cache_length,
    first_page_device,
    page_slot_table,
    cache_page_pool,
):
    holders = lax.axis_size("req")
    tensor_count = lax.axis_size("tensor")
    req_index = lax.axis_index("req")
    tensor_index = lax.axis_index("tensor")
    request_number = request_adapter.shape[0]
    cached_count = request_number // 2
    row_count = residual_input.shape[0]
    request_slot_rows = row_count // request_number
    piece_width = residual_input.shape[1]
    local_kv = key_value_weight.shape[1] // (2 * HEAD_SIZE)
    group_size = query_weight.shape[1] // (HEAD_SIZE * local_kv)
    page_rows = cache_page_pool.shape[1]
    tensor_count = lax.axis_size("tensor")
    chip_count = tensor_count // 2
    core = tensor_index % 2
    chip = tensor_index // 2
    swap = [(index, index ^ 1) for index in range(tensor_count)]
    along = [
        (2 * ((target // 2 - 1) % chip_count), target)
        if target % 2 == 0
        else (2 * ((target // 2 + 1) % chip_count) + 1, target)
        for target in range(tensor_count)
    ]
    partner = lax.ppermute(residual_input, "tensor", swap)
    pair = jnp.where(
        core == 0,
        jnp.concatenate([residual_input, partner], axis=1),
        jnp.concatenate([partner, residual_input], axis=1),
    )
    beside = lax.ppermute(pair, "tensor", along)
    relayed = lax.ppermute(
        lax.dynamic_slice_in_dim(beside, core * piece_width, piece_width, 1), "tensor", along
    )
    held = jnp.concatenate([beside, relayed], axis=1)
    mirrored = lax.ppermute(held, "tensor", swap)
    pair_width = 2 * piece_width
    minus_piece = jnp.where(core == 0, held[:, :pair_width], mirrored[:, :pair_width])
    plus_piece = jnp.where(core == 0, mirrored[:, :pair_width], held[:, :pair_width])
    opposite = jnp.where(
        core == 0,
        jnp.concatenate([held[:, pair_width:], mirrored[:, pair_width:]], axis=1),
        jnp.concatenate([mirrored[:, pair_width:], held[:, pair_width:]], axis=1),
    )
    relative = jnp.stack([pair, plus_piece, opposite, minus_piece])
    chip_order = (jnp.arange(chip_count, dtype=jnp.int32) - chip) % chip_count
    gathered = jnp.take(relative, chip_order, axis=0)
    widened = gathered.astype(jnp.float32)
    inverse = lax.rsqrt(
        jnp.sum(widened * widened, axis=(0, 2), keepdims=True) / (tensor_count * piece_width)
        + EPSILON
    )
    normed_parts = (
        widened * inverse * input_norm_gain.reshape(chip_count, 1, pair_width)
    ).astype(jnp.bfloat16)
    own_normed = (
        residual_input.astype(jnp.float32)
        * inverse[0]
        * lax.dynamic_slice_in_dim(input_norm_gain, tensor_index * piece_width, piece_width, 0)
    ).astype(jnp.bfloat16)
    adapter_parts = (
        adapter_down_maps,
        adapter_query_up,
        adapter_key_value_up,
        adapter_output_down,
        adapter_output_up,
    )
    local_adapters = adapter_down_maps.shape[0]
    flat_parts = [part.reshape(local_adapters, -1) for part in adapter_parts]
    joined = jnp.concatenate(flat_parts, axis=1)
    lane_rows = joined.shape[1] // 128
    every_adapter = lax.all_gather(
        joined.reshape(local_adapters, lane_rows, 128), "req", axis=0, tiled=True
    )
    slot_order = page_slot_table[0].reshape(holders, cached_count).T.reshape(-1)
    outgoing = cache_page_pool[slot_order].reshape(
        cached_count, holders, page_rows, cache_page_pool.shape[2]
    )
    arrived = lax.all_to_all(outgoing, "req", split_axis=1, concat_axis=1, tiled=True)
    every_adapter, arrived = lax.optimization_barrier((every_adapter, arrived))
    picked = jnp.take(every_adapter, request_adapter, axis=0, mode="clip").reshape(
        request_number, -1
    )
    picked_parts = []
    start = 0
    for part, flat in zip(adapter_parts, flat_parts):
        width = flat.shape[1]
        picked_parts.append(
            picked[:, start : start + width].reshape((request_number,) + part.shape[1:])
        )
        start += width
    down_picked, query_picked, key_value_picked, output_down_picked, oup_sel = picked_parts
    adapter_rank_size = query_picked.shape[1]
    own_columns = own_normed.reshape(request_number, request_slot_rows, piece_width)
    partial_low = jnp.einsum(
        "rsd,rkd->rsk", own_columns, down_picked, preferred_element_type=jnp.float32
    )
    reduced_input = sum_over_tensor(partial_low, tensor_count).astype(jnp.bfloat16)
    query_rows = jnp.einsum(
        "csf,cfn->sn",
        normed_parts,
        query_weight.reshape(chip_count, pair_width, -1),
        preferred_element_type=jnp.float32,
    ).reshape(request_number, request_slot_rows, -1)
    query_rows = query_rows + ADAPTER_SCALE * jnp.einsum(
        "ibm,imf->ibf",
        reduced_input[..., :adapter_rank_size],
        query_picked,
        preferred_element_type=jnp.float32,
    )
    keyval = jnp.einsum(
        "csf,cfn->sn",
        normed_parts,
        key_value_weight.reshape(chip_count, pair_width, -1),
        preferred_element_type=jnp.float32,
    ).reshape(
        request_number, request_slot_rows, local_kv, 2 * HEAD_SIZE
    )
    key_add = jnp.einsum(
        "ibm,imf->ibf",
        reduced_input[..., adapter_rank_size : 2 * adapter_rank_size],
        key_value_picked[:, 0],
        preferred_element_type=jnp.float32,
    ).reshape(request_number, request_slot_rows, local_kv, HEAD_SIZE)
    value_add = jnp.einsum(
        "ibm,imf->ibf",
        reduced_input[..., 2 * adapter_rank_size :],
        key_value_picked[:, 1],
        preferred_element_type=jnp.float32,
    ).reshape(request_number, request_slot_rows, local_kv, HEAD_SIZE)
    my_cache = lax.dynamic_slice_in_dim(cache_length, req_index * cached_count, cached_count, 0)
    offsets = jnp.stack([jnp.zeros_like(my_cache), my_cache], axis=1).reshape(request_number)
    slot_index = jnp.arange(request_slot_rows, dtype=jnp.int32)
    positions = offsets[:, None] + slot_index[None, :]
    query_rot = rotate(
        query_rows.reshape(request_number, request_slot_rows, local_kv, group_size, HEAD_SIZE),
        positions[:, :, None, None],
    ).astype(jnp.bfloat16)
    key_rot = rotate(keyval[..., :HEAD_SIZE] + key_add, positions[:, :, None]).astype(jnp.bfloat16)
    value_new = (keyval[..., HEAD_SIZE:] + value_add).astype(jnp.bfloat16)
    causal = slot_index[None, :, None] >= slot_index[None, None, :]
    own_mask = causal & (slot_index[None, None, :] < prompt_length[:, None, None])
    own_part = partial_softmax(query_rot, key_rot, value_new, own_mask)
    asked_queries = query_rot[1::2]
    my_base = lax.dynamic_slice_in_dim(first_page_device, req_index * cached_count, cached_count, 0)
    page_of = (jnp.arange(holders, dtype=jnp.int32)[None, :] - my_base[:, None]) % holders
    key_pos = (
        page_of[:, :, None] * page_rows + jnp.arange(page_rows, dtype=jnp.int32)[None, None, :]
    ).reshape(cached_count, holders * page_rows)
    entries = arrived.reshape(cached_count, holders * page_rows, local_kv, 2 * HEAD_SIZE)
    visible = jnp.broadcast_to(
        (key_pos < my_cache[:, None])[:, None, :],
        (cached_count, request_slot_rows, holders * page_rows),
    )
    cache_part = partial_softmax(
        asked_queries, entries[..., :HEAD_SIZE], entries[..., HEAD_SIZE:], visible
    )
    filler = jnp.full_like(cache_part[0], NEG_FILL)
    spread_peak = jnp.stack([filler, cache_part[0]], axis=1).reshape(own_part[0].shape)
    spread_total = jnp.stack([jnp.zeros_like(cache_part[1]), cache_part[1]], axis=1).reshape(
        own_part[1].shape
    )
    spread_sum = jnp.stack([jnp.zeros_like(cache_part[2]), cache_part[2]], axis=1).reshape(
        own_part[2].shape
    )
    highest_all = jnp.maximum(own_part[0], spread_peak)
    own_weight = jnp.exp(own_part[0] - highest_all)
    cache_weight = jnp.exp(spread_peak - highest_all)
    denominator = own_part[1] * own_weight + spread_total * cache_weight
    numerator = own_part[2] * own_weight[..., None] + spread_sum * cache_weight[..., None]
    live_rows = slot_index[None, :] < prompt_length[:, None]
    attended = jnp.where(
        live_rows[:, None, :, None, None], numerator / denominator[..., None], 0.0
    ).astype(jnp.bfloat16)
    attended = jnp.transpose(attended, (0, 2, 1, 3, 4)).reshape(row_count, -1)
    head_terms = jnp.einsum(
        "sc,ctf->tsf",
        attended,
        output_weight.reshape(output_weight.shape[0], tensor_count, piece_width),
        preferred_element_type=jnp.float32,
    )
    low_part = jnp.einsum(
        "rsc,rkc->rsk",
        attended.reshape(request_number, request_slot_rows, -1),
        output_down_picked,
        preferred_element_type=jnp.float32,
    )
    reduced_output = sum_over_tensor(low_part, tensor_count).astype(jnp.bfloat16)
    head_total = lax.psum_scatter(
        head_terms.astype(jnp.bfloat16), "tensor", scatter_dimension=0, tiled=False
    ).astype(jnp.float32)
    adapter_output = jnp.einsum(
        "ibm,imf->ibf", reduced_output, oup_sel, preferred_element_type=jnp.float32
    ).reshape(row_count, -1)
    return (head_total + ADAPTER_SCALE * adapter_output).astype(jnp.bfloat16)


def solution(mesh):
    placed = (
        P("req", "tensor"),
        P(),
        P(None, "tensor"),
        P(None, "tensor"),
        P("tensor", None),
        P("req", None, "tensor"),
        P("req", None, "tensor"),
        P("req", None, None, "tensor"),
        P("req", None, "tensor"),
        P("req", None, "tensor"),
        P("req"),
        P("req"),
        P(),
        P(),
        P("req", None),
        P("req", None, "tensor"),
    )
    return jax.shard_map(
        local, mesh=mesh, in_specs=placed, out_specs=P("req", "tensor"), check_vma=False
    )
```

```python
import jax
import jax.numpy as jnp
from jax import lax
from jax.sharding import PartitionSpec as P

HEAD_SIZE = 128


ROPE_BASE = 5000000.0
ADAPTER_SCALE = 2.0
EPSILON = 1e-05
NEG_FILL = -1e30


def rotate(vectors, positions):
    half_dim = vectors.shape[-1] // 2
    frequency = ROPE_BASE ** (-jnp.arange(half_dim, dtype=jnp.float32) / half_dim)
    angles = positions.astype(jnp.float32)[..., None] * frequency
    cosine = jnp.cos(angles)
    sine_part = jnp.sin(angles)
    front_half = vectors[..., :half_dim]
    back_half = vectors[..., half_dim:]
    return jnp.concatenate(
        [front_half * cosine - back_half * sine_part, back_half * cosine + front_half * sine_part],
        axis=-1,
    )


def partial_softmax(query_rows, key_rows, value_rows, allowed):
    score_scale = query_rows.shape[-1] ** (-0.5)
    scores = (
        jnp.einsum("bsvgd,bkvd->bvsgk", query_rows, key_rows, preferred_element_type=jnp.float32)
        * score_scale
    )
    spread_mask = allowed[:, None, :, None, :]
    scores = jnp.where(spread_mask, scores, NEG_FILL)
    peak_scores = jnp.max(scores, axis=-1)
    weights = jnp.where(spread_mask, jnp.exp(scores - peak_scores[..., None]), 0.0)
    totals = jnp.sum(weights, axis=-1)
    summed = jnp.einsum(
        "bvsgk,bkvd->bvsgd",
        weights.astype(jnp.bfloat16),
        value_rows,
        preferred_element_type=jnp.float32,
    )
    return (peak_scores, totals, summed)


def gather_by_exchange(piece, axis_name, count):
    spread = jnp.broadcast_to(piece[None], (count,) + piece.shape)
    return lax.all_to_all(spread, axis_name, split_axis=0, concat_axis=0, tiled=True)


def sum_over_tensor(partial, count):
    sent = partial.astype(jnp.bfloat16)
    position = lax.axis_index("tensor")
    received = [sent] + [
        lax.ppermute(sent, "tensor", [(index, (index + shift) % count) for index in range(count)])
        for shift in range(1, count)
    ]
    by_shift = jnp.stack(received)
    by_source = jnp.take(by_shift, (position - jnp.arange(count)) % count, axis=0)
    return by_source.astype(jnp.float32).sum(axis=0)


def local(
    residual_input,
    input_norm_gain,
    query_weight,
    key_value_weight,
    output_weight,
    adapter_down_maps,
    adapter_query_up,
    adapter_key_value_up,
    adapter_output_down,
    adapter_output_up,
    request_adapter,
    prompt_length,
    cache_length,
    first_page_device,
    page_slot_table,
    cache_page_pool,
):
    holders = lax.axis_size("req")
    tensor_count = lax.axis_size("tensor")
    req_index = lax.axis_index("req")
    tensor_index = lax.axis_index("tensor")
    request_number = request_adapter.shape[0]
    cached_count = request_number // 2
    row_count = residual_input.shape[0]
    request_slot_rows = row_count // request_number
    piece_width = residual_input.shape[1]
    local_kv = key_value_weight.shape[1] // (2 * HEAD_SIZE)
    group_size = query_weight.shape[1] // (HEAD_SIZE * local_kv)
    page_rows = cache_page_pool.shape[1]
    tensor_count = lax.axis_size("tensor")
    chip_count = tensor_count // 2
    core = tensor_index % 2
    chip = tensor_index // 2
    swap = [(index, index ^ 1) for index in range(tensor_count)]
    along = [
        (2 * ((target // 2 - 1) % chip_count), target)
        if target % 2 == 0
        else (2 * ((target // 2 + 1) % chip_count) + 1, target)
        for target in range(tensor_count)
    ]
    partner = lax.ppermute(residual_input, "tensor", swap)
    pair = jnp.where(
        core == 0,
        jnp.concatenate([residual_input, partner], axis=1),
        jnp.concatenate([partner, residual_input], axis=1),
    )
    beside = lax.ppermute(pair, "tensor", along)
    relayed = lax.ppermute(
        lax.dynamic_slice_in_dim(beside, core * piece_width, piece_width, 1), "tensor", along
    )
    held = jnp.concatenate([beside, relayed], axis=1)
    mirrored = lax.ppermute(held, "tensor", swap)
    pair_width = 2 * piece_width
    minus_piece = jnp.where(core == 0, held[:, :pair_width], mirrored[:, :pair_width])
    plus_piece = jnp.where(core == 0, mirrored[:, :pair_width], held[:, :pair_width])
    opposite = jnp.where(
        core == 0,
        jnp.concatenate([held[:, pair_width:], mirrored[:, pair_width:]], axis=1),
        jnp.concatenate([mirrored[:, pair_width:], held[:, pair_width:]], axis=1),
    )
    relative = jnp.stack([pair, plus_piece, opposite, minus_piece])
    chip_order = (jnp.arange(chip_count, dtype=jnp.int32) - chip) % chip_count
    gathered = jnp.take(relative, chip_order, axis=0)
    widened = gathered.astype(jnp.float32)
    inverse = lax.rsqrt(
        jnp.sum(widened * widened, axis=(0, 2), keepdims=True) / (tensor_count * piece_width)
        + EPSILON
    )
    normed_parts = (
        widened * inverse * input_norm_gain.reshape(chip_count, 1, pair_width)
    ).astype(jnp.bfloat16)
    own_normed = (
        residual_input.astype(jnp.float32)
        * inverse[0]
        * lax.dynamic_slice_in_dim(input_norm_gain, tensor_index * piece_width, piece_width, 0)
    ).astype(jnp.bfloat16)
    adapter_parts = (
        adapter_down_maps,
        adapter_query_up,
        adapter_key_value_up,
        adapter_output_down,
        adapter_output_up,
    )
    local_adapters = adapter_down_maps.shape[0]
    flat_parts = [part.reshape(local_adapters, -1) for part in adapter_parts]
    joined = jnp.concatenate(flat_parts, axis=1)
    lane_rows = joined.shape[1] // 128
    every_adapter = lax.all_gather(
        joined.reshape(local_adapters, lane_rows, 128), "req", axis=0, tiled=True
    )
    slot_order = page_slot_table[0].reshape(holders, cached_count).T.reshape(-1)
    outgoing = cache_page_pool[slot_order].reshape(
        cached_count, holders, page_rows, cache_page_pool.shape[2]
    )
    arrived = lax.all_to_all(outgoing, "req", split_axis=1, concat_axis=1, tiled=True)
    every_adapter, arrived = lax.optimization_barrier((every_adapter, arrived))
    picked = jnp.take(every_adapter, request_adapter, axis=0, mode="clip").reshape(
        request_number, -1
    )
    picked_parts = []
    start = 0
    for part, flat in zip(adapter_parts, flat_parts):
        width = flat.shape[1]
        picked_parts.append(
            picked[:, start : start + width].reshape((request_number,) + part.shape[1:])
        )
        start += width
    down_picked, query_picked, key_value_picked, output_down_picked, oup_sel = picked_parts
    adapter_rank_size = query_picked.shape[1]
    own_columns = own_normed.reshape(request_number, request_slot_rows, piece_width)
    partial_low = jnp.einsum(
        "rsd,rkd->rsk", own_columns, down_picked, preferred_element_type=jnp.float32
    )
    reduced_input = sum_over_tensor(partial_low, tensor_count).astype(jnp.bfloat16)
    query_rows = jnp.einsum(
        "csf,cfn->sn",
        normed_parts,
        query_weight.reshape(chip_count, pair_width, -1),
        preferred_element_type=jnp.float32,
    ).reshape(request_number, request_slot_rows, -1)
    query_rows = query_rows + ADAPTER_SCALE * jnp.einsum(
        "ibm,imf->ibf",
        reduced_input[..., :adapter_rank_size],
        query_picked,
        preferred_element_type=jnp.float32,
    )
    keyval = jnp.einsum(
        "csf,cfn->sn",
        normed_parts,
        key_value_weight.reshape(chip_count, pair_width, -1),
        preferred_element_type=jnp.float32,
    ).reshape(
        request_number, request_slot_rows, local_kv, 2 * HEAD_SIZE
    )
    key_add = jnp.einsum(
        "ibm,imf->ibf",
        reduced_input[..., adapter_rank_size : 2 * adapter_rank_size],
        key_value_picked[:, 0],
        preferred_element_type=jnp.float32,
    ).reshape(request_number, request_slot_rows, local_kv, HEAD_SIZE)
    value_add = jnp.einsum(
        "ibm,imf->ibf",
        reduced_input[..., 2 * adapter_rank_size :],
        key_value_picked[:, 1],
        preferred_element_type=jnp.float32,
    ).reshape(request_number, request_slot_rows, local_kv, HEAD_SIZE)
    my_cache = lax.dynamic_slice_in_dim(cache_length, req_index * cached_count, cached_count, 0)
    offsets = jnp.stack([jnp.zeros_like(my_cache), my_cache], axis=1).reshape(request_number)
    slot_index = jnp.arange(request_slot_rows, dtype=jnp.int32)
    positions = offsets[:, None] + slot_index[None, :]
    query_rot = rotate(
        query_rows.reshape(request_number, request_slot_rows, local_kv, group_size, HEAD_SIZE),
        positions[:, :, None, None],
    ).astype(jnp.bfloat16)
    key_rot = rotate(keyval[..., :HEAD_SIZE] + key_add, positions[:, :, None]).astype(jnp.bfloat16)
    value_new = (keyval[..., HEAD_SIZE:] + value_add).astype(jnp.bfloat16)
    causal = slot_index[None, :, None] >= slot_index[None, None, :]
    own_mask = causal & (slot_index[None, None, :] < prompt_length[:, None, None])
    own_part = partial_softmax(query_rot, key_rot, value_new, own_mask)
    asked_queries = query_rot[1::2]
    my_base = lax.dynamic_slice_in_dim(first_page_device, req_index * cached_count, cached_count, 0)
    page_of = (jnp.arange(holders, dtype=jnp.int32)[None, :] - my_base[:, None]) % holders
    key_pos = (
        page_of[:, :, None] * page_rows + jnp.arange(page_rows, dtype=jnp.int32)[None, None, :]
    ).reshape(cached_count, holders * page_rows)
    entries = arrived.reshape(cached_count, holders * page_rows, local_kv, 2 * HEAD_SIZE)
    visible = jnp.broadcast_to(
        (key_pos < my_cache[:, None])[:, None, :],
        (cached_count, request_slot_rows, holders * page_rows),
    )
    cache_part = partial_softmax(
        asked_queries, entries[..., :HEAD_SIZE], entries[..., HEAD_SIZE:], visible
    )
    filler = jnp.full_like(cache_part[0], NEG_FILL)
    spread_peak = jnp.stack([filler, cache_part[0]], axis=1).reshape(own_part[0].shape)
    spread_total = jnp.stack([jnp.zeros_like(cache_part[1]), cache_part[1]], axis=1).reshape(
        own_part[1].shape
    )
    spread_sum = jnp.stack([jnp.zeros_like(cache_part[2]), cache_part[2]], axis=1).reshape(
        own_part[2].shape
    )
    highest_all = jnp.maximum(own_part[0], spread_peak)
    own_weight = jnp.exp(own_part[0] - highest_all)
    cache_weight = jnp.exp(spread_peak - highest_all)
    denominator = own_part[1] * own_weight + spread_total * cache_weight
    numerator = own_part[2] * own_weight[..., None] + spread_sum * cache_weight[..., None]
    live_rows = slot_index[None, :] < prompt_length[:, None]
    attended = jnp.where(
        live_rows[:, None, :, None, None], numerator / denominator[..., None], 0.0
    ).astype(jnp.bfloat16)
    attended = jnp.transpose(attended, (0, 2, 1, 3, 4)).reshape(row_count, -1)
    head_terms = jnp.einsum(
        "sc,ctf->tsf",
        attended,
        output_weight.reshape(output_weight.shape[0], tensor_count, piece_width),
        preferred_element_type=jnp.float32,
    )
    low_part = jnp.einsum(
        "rsc,rkc->rsk",
        attended.reshape(request_number, request_slot_rows, -1),
        output_down_picked,
        preferred_element_type=jnp.float32,
    )
    reduced_output = sum_over_tensor(low_part, tensor_count).astype(jnp.bfloat16)
    head_total = lax.psum_scatter(
        head_terms.astype(jnp.bfloat16), "tensor", scatter_dimension=0, tiled=False
    ).astype(jnp.float32)
    adapter_output = jnp.einsum(
        "ibm,imf->ibf", reduced_output, oup_sel, preferred_element_type=jnp.float32
    ).reshape(row_count, -1)
    return (head_total + ADAPTER_SCALE * adapter_output).astype(jnp.bfloat16)


def solution(mesh):
    placed = (
        P("req", "tensor"),
        P(),
        P(None, "tensor"),
        P(None, "tensor"),
        P("tensor", None),
        P("req", None, "tensor"),
        P("req", None, "tensor"),
        P("req", None, None, "tensor"),
        P("req", None, "tensor"),
        P("req", None, "tensor"),
        P("req"),
        P("req"),
        P(),
        P(),
        P("req", None),
        P("req", None, "tensor"),
    )
    return jax.shard_map(
        local, mesh=mesh, in_specs=placed, out_specs=P("req", "tensor"), check_vma=False
    )
```

```python
import jax
import jax.numpy as jnp
from jax import lax
from jax.sharding import PartitionSpec as P

HEAD_SIZE = 128


ROPE_BASE = 5000000.0
ADAPTER_SCALE = 2.0
EPSILON = 1e-05
NEG_FILL = -1e30


def rotate(vectors, positions):
    half_dim = vectors.shape[-1] // 2
    frequency = ROPE_BASE ** (-jnp.arange(half_dim, dtype=jnp.float32) / half_dim)
    angles = positions.astype(jnp.float32)[..., None] * frequency
    cosine = jnp.cos(angles)
    sine_part = jnp.sin(angles)
    front_half = vectors[..., :half_dim]
    back_half = vectors[..., half_dim:]
    return jnp.concatenate(
        [front_half * cosine - back_half * sine_part, back_half * cosine + front_half * sine_part],
        axis=-1,
    )


def partial_softmax(query_rows, key_rows, value_rows, allowed):
    score_scale = query_rows.shape[-1] ** (-0.5)
    scores = (
        jnp.einsum("bsvgd,bkvd->bvsgk", query_rows, key_rows, preferred_element_type=jnp.float32)
        * score_scale
    )
    spread_mask = allowed[:, None, :, None, :]
    scores = jnp.where(spread_mask, scores, NEG_FILL)
    peak_scores = jnp.max(scores, axis=-1)
    weights = jnp.where(spread_mask, jnp.exp(scores - peak_scores[..., None]), 0.0)
    totals = jnp.sum(weights, axis=-1)
    summed = jnp.einsum(
        "bvsgk,bkvd->bvsgd",
        weights.astype(jnp.bfloat16),
        value_rows,
        preferred_element_type=jnp.float32,
    )
    return (peak_scores, totals, summed)


def gather_by_exchange(piece, axis_name, count):
    spread = jnp.broadcast_to(piece[None], (count,) + piece.shape)
    return lax.all_to_all(spread, axis_name, split_axis=0, concat_axis=0, tiled=True)


def sum_over_tensor(partial, count):
    total = partial.astype(jnp.bfloat16).astype(jnp.float32)
    step = 1
    while step < count:
        pairs = [(index, index ^ step) for index in range(count)]
        sent = total.astype(jnp.bfloat16)
        total = sent.astype(jnp.float32) + lax.ppermute(sent, "tensor", pairs).astype(jnp.float32)
        step *= 2
    return total


def local(
    residual_input,
    input_norm_gain,
    query_weight,
    key_value_weight,
    output_weight,
    adapter_down_maps,
    adapter_query_up,
    adapter_key_value_up,
    adapter_output_down,
    adapter_output_up,
    request_adapter,
    prompt_length,
    cache_length,
    first_page_device,
    page_slot_table,
    cache_page_pool,
):
    holders = lax.axis_size("req")
    tensor_count = lax.axis_size("tensor")
    req_index = lax.axis_index("req")
    tensor_index = lax.axis_index("tensor")
    request_number = request_adapter.shape[0]
    cached_count = request_number // 2
    row_count = residual_input.shape[0]
    request_slot_rows = row_count // request_number
    piece_width = residual_input.shape[1]
    local_kv = key_value_weight.shape[1] // (2 * HEAD_SIZE)
    group_size = query_weight.shape[1] // (HEAD_SIZE * local_kv)
    page_rows = cache_page_pool.shape[1]
    tensor_count = lax.axis_size("tensor")
    chip_count = tensor_count // 2
    core = tensor_index % 2
    chip = tensor_index // 2
    swap = [(index, index ^ 1) for index in range(tensor_count)]
    along = [
        (2 * ((target // 2 - 1) % chip_count), target)
        if target % 2 == 0
        else (2 * ((target // 2 + 1) % chip_count) + 1, target)
        for target in range(tensor_count)
    ]
    partner = lax.ppermute(residual_input, "tensor", swap)
    pair = jnp.concatenate([residual_input, partner], axis=1)
    beside = lax.ppermute(pair, "tensor", along)
    relayed = lax.ppermute(beside[:, :piece_width], "tensor", along)
    held = jnp.concatenate([beside, relayed], axis=1)
    mirrored = lax.ppermute(held, "tensor", swap)
    pair_width = 2 * piece_width
    widened = jnp.concatenate(
        [pair, held[:, :pair_width], mirrored[:, :pair_width], relayed, mirrored[:, pair_width:]],
        axis=1,
    ).astype(jnp.float32)
    near = (chip - 1 + 2 * core) % chip_count
    far = (chip + 1 - 2 * core) % chip_count
    across = (chip + 2) % chip_count
    block_ids = jnp.stack(
        [
            tensor_index,
            tensor_index ^ 1,
            2 * near + core,
            2 * near + 1 - core,
            2 * far + 1 - core,
            2 * far + core,
            2 * across + core,
            2 * across + 1 - core,
        ]
    )
    inverse = lax.rsqrt(jnp.mean(widened * widened, axis=1, keepdims=True) + EPSILON)
    local_gain = jnp.take(
        input_norm_gain.reshape(tensor_count, piece_width), block_ids, axis=0, mode="clip"
    ).reshape(-1)
    normed = (widened * inverse * local_gain).astype(jnp.bfloat16)

    def local_rows(weight):
        return jnp.take(
            weight.reshape(tensor_count, piece_width, weight.shape[1]), block_ids, axis=0, mode="clip"
        ).reshape(weight.shape)

    adapter_parts = (
        adapter_down_maps,
        adapter_query_up,
        adapter_key_value_up,
        adapter_output_down,
        adapter_output_up,
    )
    local_adapters = adapter_down_maps.shape[0]
    flat_parts = [part.reshape(local_adapters, -1) for part in adapter_parts]
    joined = jnp.concatenate(flat_parts, axis=1)
    lane_rows = joined.shape[1] // 128
    every_adapter = lax.all_gather(
        joined.reshape(local_adapters, lane_rows, 128), "req", axis=0, tiled=True
    )
    slot_order = page_slot_table[0].reshape(holders, cached_count).T.reshape(-1)
    outgoing = cache_page_pool[slot_order].reshape(
        cached_count, holders, page_rows, cache_page_pool.shape[2]
    )
    arrived = lax.all_to_all(outgoing, "req", split_axis=1, concat_axis=1, tiled=True)
    every_adapter, arrived = lax.optimization_barrier((every_adapter, arrived))
    picked = jnp.take(every_adapter, request_adapter, axis=0, mode="clip").reshape(
        request_number, -1
    )
    picked_parts = []
    start = 0
    for part, flat in zip(adapter_parts, flat_parts):
        width = flat.shape[1]
        picked_parts.append(
            picked[:, start : start + width].reshape((request_number,) + part.shape[1:])
        )
        start += width
    down_picked, query_picked, key_value_picked, output_down_picked, oup_sel = picked_parts
    adapter_rank_size = query_picked.shape[1]
    own_columns = normed[:, :piece_width].reshape(request_number, request_slot_rows, piece_width)
    partial_low = jnp.einsum(
        "rsd,rkd->rsk", own_columns, down_picked, preferred_element_type=jnp.float32
    )
    reduced_input = sum_over_tensor(partial_low, tensor_count).astype(jnp.bfloat16)
    query_rows = jnp.dot(normed, local_rows(query_weight), preferred_element_type=jnp.float32).reshape(request_number, request_slot_rows, -1)
    query_rows = query_rows + ADAPTER_SCALE * jnp.einsum(
        "ibm,imf->ibf",
        reduced_input[..., :adapter_rank_size],
        query_picked,
        preferred_element_type=jnp.float32,
    )
    keyval = jnp.dot(normed, local_rows(key_value_weight), preferred_element_type=jnp.float32).reshape(
        request_number, request_slot_rows, local_kv, 2 * HEAD_SIZE
    )
    key_add = jnp.einsum(
        "ibm,imf->ibf",
        reduced_input[..., adapter_rank_size : 2 * adapter_rank_size],
        key_value_picked[:, 0],
        preferred_element_type=jnp.float32,
    ).reshape(request_number, request_slot_rows, local_kv, HEAD_SIZE)
    value_add = jnp.einsum(
        "ibm,imf->ibf",
        reduced_input[..., 2 * adapter_rank_size :],
        key_value_picked[:, 1],
        preferred_element_type=jnp.float32,
    ).reshape(request_number, request_slot_rows, local_kv, HEAD_SIZE)
    my_cache = lax.dynamic_slice_in_dim(cache_length, req_index * cached_count, cached_count, 0)
    offsets = jnp.stack([jnp.zeros_like(my_cache), my_cache], axis=1).reshape(request_number)
    slot_index = jnp.arange(request_slot_rows, dtype=jnp.int32)
    positions = offsets[:, None] + slot_index[None, :]
    query_rot = rotate(
        query_rows.reshape(request_number, request_slot_rows, local_kv, group_size, HEAD_SIZE),
        positions[:, :, None, None],
    ).astype(jnp.bfloat16)
    key_rot = rotate(keyval[..., :HEAD_SIZE] + key_add, positions[:, :, None]).astype(jnp.bfloat16)
    value_new = (keyval[..., HEAD_SIZE:] + value_add).astype(jnp.bfloat16)
    causal = slot_index[None, :, None] >= slot_index[None, None, :]
    own_mask = causal & (slot_index[None, None, :] < prompt_length[:, None, None])
    own_part = partial_softmax(query_rot, key_rot, value_new, own_mask)
    asked_queries = query_rot[1::2]
    my_base = lax.dynamic_slice_in_dim(first_page_device, req_index * cached_count, cached_count, 0)
    page_of = (jnp.arange(holders, dtype=jnp.int32)[None, :] - my_base[:, None]) % holders
    key_pos = (
        page_of[:, :, None] * page_rows + jnp.arange(page_rows, dtype=jnp.int32)[None, None, :]
    ).reshape(cached_count, holders * page_rows)
    entries = arrived.reshape(cached_count, holders * page_rows, local_kv, 2 * HEAD_SIZE)
    visible = jnp.broadcast_to(
        (key_pos < my_cache[:, None])[:, None, :],
        (cached_count, request_slot_rows, holders * page_rows),
    )
    cache_part = partial_softmax(
        asked_queries, entries[..., :HEAD_SIZE], entries[..., HEAD_SIZE:], visible
    )
    filler = jnp.full_like(cache_part[0], NEG_FILL)
    spread_peak = jnp.stack([filler, cache_part[0]], axis=1).reshape(own_part[0].shape)
    spread_total = jnp.stack([jnp.zeros_like(cache_part[1]), cache_part[1]], axis=1).reshape(
        own_part[1].shape
    )
    spread_sum = jnp.stack([jnp.zeros_like(cache_part[2]), cache_part[2]], axis=1).reshape(
        own_part[2].shape
    )
    highest_all = jnp.maximum(own_part[0], spread_peak)
    own_weight = jnp.exp(own_part[0] - highest_all)
    cache_weight = jnp.exp(spread_peak - highest_all)
    denominator = own_part[1] * own_weight + spread_total * cache_weight
    numerator = own_part[2] * own_weight[..., None] + spread_sum * cache_weight[..., None]
    live_rows = slot_index[None, :] < prompt_length[:, None]
    attended = jnp.where(
        live_rows[:, None, :, None, None], numerator / denominator[..., None], 0.0
    ).astype(jnp.bfloat16)
    attended = jnp.transpose(attended, (0, 2, 1, 3, 4)).reshape(row_count, -1)
    head_terms = jnp.einsum(
        "sc,ctf->tsf",
        attended,
        output_weight.reshape(output_weight.shape[0], tensor_count, piece_width),
        preferred_element_type=jnp.float32,
    )
    low_part = jnp.einsum(
        "rsc,rkc->rsk",
        attended.reshape(request_number, request_slot_rows, -1),
        output_down_picked,
        preferred_element_type=jnp.float32,
    )
    reduced_output = sum_over_tensor(low_part, tensor_count).astype(jnp.bfloat16)
    head_total = lax.psum_scatter(
        head_terms.astype(jnp.bfloat16), "tensor", scatter_dimension=0, tiled=False
    ).astype(jnp.float32)
    adapter_output = jnp.einsum(
        "ibm,imf->ibf", reduced_output, oup_sel, preferred_element_type=jnp.float32
    ).reshape(row_count, -1)
    return (head_total + ADAPTER_SCALE * adapter_output).astype(jnp.bfloat16)


def solution(mesh):
    placed = (
        P("req", "tensor"),
        P(),
        P(None, "tensor"),
        P(None, "tensor"),
        P("tensor", None),
        P("req", None, "tensor"),
        P("req", None, "tensor"),
        P("req", None, None, "tensor"),
        P("req", None, "tensor"),
        P("req", None, "tensor"),
        P("req"),
        P("req"),
        P(),
        P(),
        P("req", None),
        P("req", None, "tensor"),
    )
    return jax.shard_map(
        local, mesh=mesh, in_specs=placed, out_specs=P("req", "tensor"), check_vma=False
    )
```

```python
import jax
import jax.numpy as jnp
from jax import lax
from jax.sharding import PartitionSpec as P

HEAD_SIZE = 128


ROPE_BASE = 5000000.0
ADAPTER_SCALE = 2.0
EPSILON = 1e-05
NEG_FILL = -1e30


def rotate(vectors, positions):
    half_dim = vectors.shape[-1] // 2
    frequency = ROPE_BASE ** (-jnp.arange(half_dim, dtype=jnp.float32) / half_dim)
    angles = positions.astype(jnp.float32)[..., None] * frequency
    cosine = jnp.cos(angles)
    sine_part = jnp.sin(angles)
    front_half = vectors[..., :half_dim]
    back_half = vectors[..., half_dim:]
    return jnp.concatenate(
        [front_half * cosine - back_half * sine_part, back_half * cosine + front_half * sine_part],
        axis=-1,
    )


def partial_softmax(query_rows, key_rows, value_rows, allowed):
    score_scale = query_rows.shape[-1] ** (-0.5)
    scores = (
        jnp.einsum("bsvgd,bkvd->bvsgk", query_rows, key_rows, preferred_element_type=jnp.float32)
        * score_scale
    )
    spread_mask = allowed[:, None, :, None, :]
    scores = jnp.where(spread_mask, scores, NEG_FILL)
    peak_scores = jnp.max(scores, axis=-1)
    weights = jnp.where(spread_mask, jnp.exp(scores - peak_scores[..., None]), 0.0)
    totals = jnp.sum(weights, axis=-1)
    summed = jnp.einsum(
        "bvsgk,bkvd->bvsgd",
        weights.astype(jnp.bfloat16),
        value_rows,
        preferred_element_type=jnp.float32,
    )
    return (peak_scores, totals, summed)


def gather_by_exchange(piece, axis_name, count):
    spread = jnp.broadcast_to(piece[None], (count,) + piece.shape)
    return lax.all_to_all(spread, axis_name, split_axis=0, concat_axis=0, tiled=True)


def sum_over_tensor(partial, count):
    total = partial.astype(jnp.bfloat16).astype(jnp.float32)
    step = 1
    while step < count:
        pairs = [(index, index ^ step) for index in range(count)]
        sent = total.astype(jnp.bfloat16)
        total = sent.astype(jnp.float32) + lax.ppermute(sent, "tensor", pairs).astype(jnp.float32)
        step *= 2
    return total


def local(
    residual_input,
    input_norm_gain,
    query_weight,
    key_value_weight,
    output_weight,
    adapter_down_maps,
    adapter_query_up,
    adapter_key_value_up,
    adapter_output_down,
    adapter_output_up,
    request_adapter,
    prompt_length,
    cache_length,
    first_page_device,
    page_slot_table,
    cache_page_pool,
):
    holders = lax.axis_size("req")
    tensor_count = lax.axis_size("tensor")
    req_index = lax.axis_index("req")
    tensor_index = lax.axis_index("tensor")
    request_number = request_adapter.shape[0]
    cached_count = request_number // 2
    row_count = residual_input.shape[0]
    request_slot_rows = row_count // request_number
    piece_width = residual_input.shape[1]
    local_kv = key_value_weight.shape[1] // (2 * HEAD_SIZE)
    group_size = query_weight.shape[1] // (HEAD_SIZE * local_kv)
    page_rows = cache_page_pool.shape[1]
    tensor_count = lax.axis_size("tensor")
    chip_count = tensor_count // 2
    core = tensor_index % 2
    chip = tensor_index // 2
    swap = [(index, index ^ 1) for index in range(tensor_count)]
    along = [
        (2 * ((target // 2 - 1) % chip_count), target)
        if target % 2 == 0
        else (2 * ((target // 2 + 1) % chip_count) + 1, target)
        for target in range(tensor_count)
    ]
    partner = lax.ppermute(residual_input, "tensor", swap)
    pair = jnp.where(
        core == 0,
        jnp.concatenate([residual_input, partner], axis=1),
        jnp.concatenate([partner, residual_input], axis=1),
    )
    beside = lax.ppermute(pair, "tensor", along)
    relayed = lax.ppermute(
        lax.dynamic_slice_in_dim(beside, core * piece_width, piece_width, 1), "tensor", along
    )
    held = jnp.concatenate([beside, relayed], axis=1)
    mirrored = lax.ppermute(held, "tensor", swap)
    pair_width = 2 * piece_width
    minus_piece = jnp.where(core == 0, held[:, :pair_width], mirrored[:, :pair_width])
    plus_piece = jnp.where(core == 0, mirrored[:, :pair_width], held[:, :pair_width])
    opposite = jnp.where(
        core == 0,
        jnp.concatenate([held[:, pair_width:], mirrored[:, pair_width:]], axis=1),
        jnp.concatenate([mirrored[:, pair_width:], held[:, pair_width:]], axis=1),
    )
    relative = jnp.stack([pair, plus_piece, opposite, minus_piece])
    chip_order = (jnp.arange(chip_count, dtype=jnp.int32) - chip) % chip_count
    gathered = jnp.take(relative, chip_order, axis=0)
    widened = gathered.astype(jnp.float32)
    inverse = lax.rsqrt(
        jnp.sum(widened * widened, axis=(0, 2), keepdims=True) / (tensor_count * piece_width)
        + EPSILON
    )
    normed_parts = (
        widened * inverse * input_norm_gain.reshape(chip_count, 1, pair_width)
    ).astype(jnp.bfloat16)
    own_normed = (
        residual_input.astype(jnp.float32)
        * inverse[0]
        * lax.dynamic_slice_in_dim(input_norm_gain, tensor_index * piece_width, piece_width, 0)
    ).astype(jnp.bfloat16)
    adapter_parts = (
        adapter_down_maps,
        adapter_query_up,
        adapter_key_value_up,
        adapter_output_down,
        adapter_output_up,
    )
    local_adapters = adapter_down_maps.shape[0]
    flat_parts = [part.reshape(local_adapters, -1) for part in adapter_parts]
    joined = jnp.concatenate(flat_parts, axis=1)
    lane_rows = joined.shape[1] // 128
    every_adapter = lax.all_gather(
        joined.reshape(local_adapters, lane_rows, 128), "req", axis=0, tiled=True
    )
    slot_order = page_slot_table[0].reshape(holders, cached_count).T.reshape(-1)
    outgoing = cache_page_pool[slot_order].reshape(
        cached_count, holders, page_rows, cache_page_pool.shape[2]
    )
    arrived = lax.all_to_all(outgoing, "req", split_axis=1, concat_axis=1, tiled=True)
    every_adapter, arrived = lax.optimization_barrier((every_adapter, arrived))
    picked = jnp.take(every_adapter, request_adapter, axis=0, mode="clip").reshape(
        request_number, -1
    )
    picked_parts = []
    start = 0
    for part, flat in zip(adapter_parts, flat_parts):
        width = flat.shape[1]
        picked_parts.append(
            picked[:, start : start + width].reshape((request_number,) + part.shape[1:])
        )
        start += width
    down_picked, query_picked, key_value_picked, output_down_picked, oup_sel = picked_parts
    adapter_rank_size = query_picked.shape[1]
    own_columns = own_normed.reshape(request_number, request_slot_rows, piece_width)
    partial_low = jnp.einsum(
        "rsd,rkd->rsk", own_columns, down_picked, preferred_element_type=jnp.float32
    )
    reduced_input = sum_over_tensor(partial_low, tensor_count).astype(jnp.bfloat16)
    query_rows = jnp.einsum(
        "csf,cfn->sn",
        normed_parts,
        query_weight.reshape(chip_count, pair_width, -1),
        preferred_element_type=jnp.float32,
    ).reshape(request_number, request_slot_rows, -1)
    query_rows = query_rows + ADAPTER_SCALE * jnp.einsum(
        "ibm,imf->ibf",
        reduced_input[..., :adapter_rank_size],
        query_picked,
        preferred_element_type=jnp.float32,
    )
    keyval = jnp.einsum(
        "csf,cfn->sn",
        normed_parts,
        key_value_weight.reshape(chip_count, pair_width, -1),
        preferred_element_type=jnp.float32,
    ).reshape(
        request_number, request_slot_rows, local_kv, 2 * HEAD_SIZE
    )
    key_add = jnp.einsum(
        "ibm,imf->ibf",
        reduced_input[..., adapter_rank_size : 2 * adapter_rank_size],
        key_value_picked[:, 0],
        preferred_element_type=jnp.float32,
    ).reshape(request_number, request_slot_rows, local_kv, HEAD_SIZE)
    value_add = jnp.einsum(
        "ibm,imf->ibf",
        reduced_input[..., 2 * adapter_rank_size :],
        key_value_picked[:, 1],
        preferred_element_type=jnp.float32,
    ).reshape(request_number, request_slot_rows, local_kv, HEAD_SIZE)
    my_cache = lax.dynamic_slice_in_dim(cache_length, req_index * cached_count, cached_count, 0)
    offsets = jnp.stack([jnp.zeros_like(my_cache), my_cache], axis=1).reshape(request_number)
    slot_index = jnp.arange(request_slot_rows, dtype=jnp.int32)
    positions = offsets[:, None] + slot_index[None, :]
    query_rot = rotate(
        query_rows.reshape(request_number, request_slot_rows, local_kv, group_size, HEAD_SIZE),
        positions[:, :, None, None],
    ).astype(jnp.bfloat16)
    key_rot = rotate(keyval[..., :HEAD_SIZE] + key_add, positions[:, :, None]).astype(jnp.bfloat16)
    value_new = (keyval[..., HEAD_SIZE:] + value_add).astype(jnp.bfloat16)
    causal = slot_index[None, :, None] >= slot_index[None, None, :]
    own_mask = causal & (slot_index[None, None, :] < prompt_length[:, None, None])
    own_part = partial_softmax(query_rot, key_rot, value_new, own_mask)
    asked_queries = query_rot[1::2]
    my_base = lax.dynamic_slice_in_dim(first_page_device, req_index * cached_count, cached_count, 0)
    page_of = (jnp.arange(holders, dtype=jnp.int32)[None, :] - my_base[:, None]) % holders
    key_pos = (
        page_of[:, :, None] * page_rows + jnp.arange(page_rows, dtype=jnp.int32)[None, None, :]
    ).reshape(cached_count, holders * page_rows)
    entries = arrived.reshape(cached_count, holders * page_rows, local_kv, 2 * HEAD_SIZE)
    visible = jnp.broadcast_to(
        (key_pos < my_cache[:, None])[:, None, :],
        (cached_count, request_slot_rows, holders * page_rows),
    )
    cache_part = partial_softmax(
        asked_queries, entries[..., :HEAD_SIZE], entries[..., HEAD_SIZE:], visible
    )
    filler = jnp.full_like(cache_part[0], NEG_FILL)
    spread_peak = jnp.stack([filler, cache_part[0]], axis=1).reshape(own_part[0].shape)
    spread_total = jnp.stack([jnp.zeros_like(cache_part[1]), cache_part[1]], axis=1).reshape(
        own_part[1].shape
    )
    spread_sum = jnp.stack([jnp.zeros_like(cache_part[2]), cache_part[2]], axis=1).reshape(
        own_part[2].shape
    )
    highest_all = jnp.maximum(own_part[0], spread_peak)
    own_weight = jnp.exp(own_part[0] - highest_all)
    cache_weight = jnp.exp(spread_peak - highest_all)
    denominator = own_part[1] * own_weight + spread_total * cache_weight
    numerator = own_part[2] * own_weight[..., None] + spread_sum * cache_weight[..., None]
    live_rows = slot_index[None, :] < prompt_length[:, None]
    attended = jnp.where(
        live_rows[:, None, :, None, None], numerator / denominator[..., None], 0.0
    ).astype(jnp.bfloat16)
    attended = jnp.transpose(attended, (0, 2, 1, 3, 4)).reshape(row_count, -1)
    head_terms = jnp.einsum(
        "sc,ctf->tsf",
        attended,
        output_weight.reshape(output_weight.shape[0], tensor_count, piece_width),
        preferred_element_type=jnp.float32,
    )
    low_part = jnp.einsum(
        "rsc,rkc->rsk",
        attended.reshape(request_number, request_slot_rows, -1),
        output_down_picked,
        preferred_element_type=jnp.float32,
    )
    reduced_output = sum_over_tensor(low_part, tensor_count).astype(jnp.bfloat16)
    by_chip = head_terms.astype(jnp.bfloat16).reshape(
        (chip_count, 2) + head_terms.shape[1:]
    )
    kept = lax.dynamic_index_in_dim(by_chip, core, 1, keepdims=False)
    given = lax.dynamic_index_in_dim(by_chip, 1 - core, 1, keepdims=False)
    chip_total = (
        kept.astype(jnp.float32)
        + lax.ppermute(given, "tensor", swap).astype(jnp.float32)
    ).astype(jnp.bfloat16)
    same_core = [list(range(side, tensor_count, 2)) for side in range(2)]
    head_total = lax.psum_scatter(
        chip_total, "tensor", scatter_dimension=0, axis_index_groups=same_core, tiled=False
    ).astype(jnp.float32)
    adapter_output = jnp.einsum(
        "ibm,imf->ibf", reduced_output, oup_sel, preferred_element_type=jnp.float32
    ).reshape(row_count, -1)
    return (head_total + ADAPTER_SCALE * adapter_output).astype(jnp.bfloat16)


def solution(mesh):
    placed = (
        P("req", "tensor"),
        P(),
        P(None, "tensor"),
        P(None, "tensor"),
        P("tensor", None),
        P("req", None, "tensor"),
        P("req", None, "tensor"),
        P("req", None, None, "tensor"),
        P("req", None, "tensor"),
        P("req", None, "tensor"),
        P("req"),
        P("req"),
        P(),
        P(),
        P("req", None),
        P("req", None, "tensor"),
    )
    return jax.shard_map(
        local, mesh=mesh, in_specs=placed, out_specs=P("req", "tensor"), check_vma=False
    )
```

```python
import jax
import jax.numpy as jnp
from jax import lax
from jax.sharding import PartitionSpec as P

HEAD_SIZE = 128


ROPE_BASE = 5000000.0
ADAPTER_SCALE = 2.0
EPSILON = 1e-05
NEG_FILL = -1e30


def rotate(vectors, positions):
    half_dim = vectors.shape[-1] // 2
    frequency = ROPE_BASE ** (-jnp.arange(half_dim, dtype=jnp.float32) / half_dim)
    angles = positions.astype(jnp.float32)[..., None] * frequency
    cosine = jnp.cos(angles)
    sine_part = jnp.sin(angles)
    front_half = vectors[..., :half_dim]
    back_half = vectors[..., half_dim:]
    return jnp.concatenate(
        [front_half * cosine - back_half * sine_part, back_half * cosine + front_half * sine_part],
        axis=-1,
    )


def partial_softmax(query_rows, key_rows, value_rows, allowed):
    score_scale = query_rows.shape[-1] ** (-0.5)
    scores = (
        jnp.einsum("bsvgd,bkvd->bvsgk", query_rows, key_rows, preferred_element_type=jnp.float32)
        * score_scale
    )
    spread_mask = allowed[:, None, :, None, :]
    scores = jnp.where(spread_mask, scores, NEG_FILL)
    peak_scores = jnp.max(scores, axis=-1)
    weights = jnp.where(spread_mask, jnp.exp(scores - peak_scores[..., None]), 0.0)
    totals = jnp.sum(weights, axis=-1)
    summed = jnp.einsum(
        "bvsgk,bkvd->bvsgd",
        weights.astype(jnp.bfloat16),
        value_rows,
        preferred_element_type=jnp.float32,
    )
    return (peak_scores, totals, summed)


def gather_by_exchange(piece, axis_name, count):
    spread = jnp.broadcast_to(piece[None], (count,) + piece.shape)
    return lax.all_to_all(spread, axis_name, split_axis=0, concat_axis=0, tiled=True)


def sum_over_tensor(partial, count):
    total = partial.astype(jnp.bfloat16).astype(jnp.float32)
    step = 1
    while step < count:
        pairs = [(index, index ^ step) for index in range(count)]
        sent = total.astype(jnp.bfloat16)
        total = sent.astype(jnp.float32) + lax.ppermute(sent, "tensor", pairs).astype(jnp.float32)
        step *= 2
    return total


def local(
    residual_input,
    input_norm_gain,
    query_weight,
    key_value_weight,
    output_weight,
    adapter_down_maps,
    adapter_query_up,
    adapter_key_value_up,
    adapter_output_down,
    adapter_output_up,
    request_adapter,
    prompt_length,
    cache_length,
    first_page_device,
    page_slot_table,
    cache_page_pool,
):
    holders = lax.axis_size("req")
    tensor_count = lax.axis_size("tensor")
    req_index = lax.axis_index("req")
    tensor_index = lax.axis_index("tensor")
    request_number = request_adapter.shape[0]
    cached_count = request_number // 2
    row_count = residual_input.shape[0]
    request_slot_rows = row_count // request_number
    piece_width = residual_input.shape[1]
    local_kv = key_value_weight.shape[1] // (2 * HEAD_SIZE)
    group_size = query_weight.shape[1] // (HEAD_SIZE * local_kv)
    page_rows = cache_page_pool.shape[1]
    tensor_count = lax.axis_size("tensor")
    chip_count = tensor_count // 2
    core = tensor_index % 2
    chip = tensor_index // 2
    swap = [(index, index ^ 1) for index in range(tensor_count)]
    along = [
        (2 * ((target // 2 - 1) % chip_count), target)
        if target % 2 == 0
        else (2 * ((target // 2 + 1) % chip_count) + 1, target)
        for target in range(tensor_count)
    ]
    partner = lax.ppermute(residual_input, "tensor", swap)
    pair = jnp.where(
        core == 0,
        jnp.concatenate([residual_input, partner], axis=1),
        jnp.concatenate([partner, residual_input], axis=1),
    )
    beside = lax.ppermute(pair, "tensor", along)
    relayed = lax.ppermute(
        lax.dynamic_slice_in_dim(beside, core * piece_width, piece_width, 1), "tensor", along
    )
    held = jnp.concatenate([beside, relayed], axis=1)
    mirrored = lax.ppermute(held, "tensor", swap)
    pair_width = 2 * piece_width
    minus_piece = jnp.where(core == 0, held[:, :pair_width], mirrored[:, :pair_width])
    plus_piece = jnp.where(core == 0, mirrored[:, :pair_width], held[:, :pair_width])
    opposite = jnp.where(
        core == 0,
        jnp.concatenate([held[:, pair_width:], mirrored[:, pair_width:]], axis=1),
        jnp.concatenate([mirrored[:, pair_width:], held[:, pair_width:]], axis=1),
    )
    relative = jnp.stack([pair, plus_piece, opposite, minus_piece])
    chip_order = (jnp.arange(chip_count, dtype=jnp.int32) - chip) % chip_count
    gathered = jnp.take(relative, chip_order, axis=0)
    widened = gathered.astype(jnp.float32)
    inverse = lax.rsqrt(
        jnp.sum(widened * widened, axis=(0, 2), keepdims=True) / (tensor_count * piece_width)
        + EPSILON
    )
    normed_parts = (
        widened * inverse * input_norm_gain.reshape(chip_count, 1, pair_width)
    ).astype(jnp.bfloat16)
    own_normed = (
        residual_input.astype(jnp.float32)
        * inverse[0]
        * lax.dynamic_slice_in_dim(input_norm_gain, tensor_index * piece_width, piece_width, 0)
    ).astype(jnp.bfloat16)
    adapter_parts = (
        adapter_down_maps,
        adapter_query_up,
        adapter_key_value_up,
        adapter_output_down,
        adapter_output_up,
    )
    local_adapters = adapter_down_maps.shape[0]
    flat_parts = [part.reshape(local_adapters, -1) for part in adapter_parts]
    joined = jnp.concatenate(flat_parts, axis=1)
    lane_rows = joined.shape[1] // 128
    every_adapter = lax.all_gather(
        joined.reshape(local_adapters, lane_rows, 128), "req", axis=0, tiled=True
    )
    slot_order = page_slot_table[0].reshape(holders, cached_count).T.reshape(-1)
    outgoing = cache_page_pool[slot_order].reshape(
        cached_count, holders, page_rows, cache_page_pool.shape[2]
    )
    arrived = lax.all_to_all(outgoing, "req", split_axis=1, concat_axis=1, tiled=True)
    every_adapter, arrived = lax.optimization_barrier((every_adapter, arrived))
    picked = jnp.stack(
        [
            lax.dynamic_index_in_dim(every_adapter, request_adapter[slot], 0, keepdims=False)
            for slot in range(request_number)
        ]
    ).reshape(request_number, -1)
    picked_parts = []
    start = 0
    for part, flat in zip(adapter_parts, flat_parts):
        width = flat.shape[1]
        picked_parts.append(
            picked[:, start : start + width].reshape((request_number,) + part.shape[1:])
        )
        start += width
    down_picked, query_picked, key_value_picked, output_down_picked, oup_sel = picked_parts
    adapter_rank_size = query_picked.shape[1]
    own_columns = own_normed.reshape(request_number, request_slot_rows, piece_width)
    partial_low = jnp.einsum(
        "rsd,rkd->rsk", own_columns, down_picked, preferred_element_type=jnp.float32
    )
    reduced_input = sum_over_tensor(partial_low, tensor_count).astype(jnp.bfloat16)
    query_rows = jnp.einsum(
        "csf,cfn->sn",
        normed_parts,
        query_weight.reshape(chip_count, pair_width, -1),
        preferred_element_type=jnp.float32,
    ).reshape(request_number, request_slot_rows, -1)
    query_rows = query_rows + ADAPTER_SCALE * jnp.einsum(
        "ibm,imf->ibf",
        reduced_input[..., :adapter_rank_size],
        query_picked,
        preferred_element_type=jnp.float32,
    )
    keyval = jnp.einsum(
        "csf,cfn->sn",
        normed_parts,
        key_value_weight.reshape(chip_count, pair_width, -1),
        preferred_element_type=jnp.float32,
    ).reshape(
        request_number, request_slot_rows, local_kv, 2 * HEAD_SIZE
    )
    key_add = jnp.einsum(
        "ibm,imf->ibf",
        reduced_input[..., adapter_rank_size : 2 * adapter_rank_size],
        key_value_picked[:, 0],
        preferred_element_type=jnp.float32,
    ).reshape(request_number, request_slot_rows, local_kv, HEAD_SIZE)
    value_add = jnp.einsum(
        "ibm,imf->ibf",
        reduced_input[..., 2 * adapter_rank_size :],
        key_value_picked[:, 1],
        preferred_element_type=jnp.float32,
    ).reshape(request_number, request_slot_rows, local_kv, HEAD_SIZE)
    my_cache = lax.dynamic_slice_in_dim(cache_length, req_index * cached_count, cached_count, 0)
    offsets = jnp.stack([jnp.zeros_like(my_cache), my_cache], axis=1).reshape(request_number)
    slot_index = jnp.arange(request_slot_rows, dtype=jnp.int32)
    positions = offsets[:, None] + slot_index[None, :]
    query_rot = rotate(
        query_rows.reshape(request_number, request_slot_rows, local_kv, group_size, HEAD_SIZE),
        positions[:, :, None, None],
    ).astype(jnp.bfloat16)
    key_rot = rotate(keyval[..., :HEAD_SIZE] + key_add, positions[:, :, None]).astype(jnp.bfloat16)
    value_new = (keyval[..., HEAD_SIZE:] + value_add).astype(jnp.bfloat16)
    causal = slot_index[None, :, None] >= slot_index[None, None, :]
    own_mask = causal & (slot_index[None, None, :] < prompt_length[:, None, None])
    own_part = partial_softmax(query_rot, key_rot, value_new, own_mask)
    asked_queries = query_rot[1::2]
    my_base = lax.dynamic_slice_in_dim(first_page_device, req_index * cached_count, cached_count, 0)
    page_of = (jnp.arange(holders, dtype=jnp.int32)[None, :] - my_base[:, None]) % holders
    key_pos = (
        page_of[:, :, None] * page_rows + jnp.arange(page_rows, dtype=jnp.int32)[None, None, :]
    ).reshape(cached_count, holders * page_rows)
    entries = arrived.reshape(cached_count, holders * page_rows, local_kv, 2 * HEAD_SIZE)
    visible = jnp.broadcast_to(
        (key_pos < my_cache[:, None])[:, None, :],
        (cached_count, request_slot_rows, holders * page_rows),
    )
    cache_part = partial_softmax(
        asked_queries, entries[..., :HEAD_SIZE], entries[..., HEAD_SIZE:], visible
    )
    filler = jnp.full_like(cache_part[0], NEG_FILL)
    spread_peak = jnp.stack([filler, cache_part[0]], axis=1).reshape(own_part[0].shape)
    spread_total = jnp.stack([jnp.zeros_like(cache_part[1]), cache_part[1]], axis=1).reshape(
        own_part[1].shape
    )
    spread_sum = jnp.stack([jnp.zeros_like(cache_part[2]), cache_part[2]], axis=1).reshape(
        own_part[2].shape
    )
    highest_all = jnp.maximum(own_part[0], spread_peak)
    own_weight = jnp.exp(own_part[0] - highest_all)
    cache_weight = jnp.exp(spread_peak - highest_all)
    denominator = own_part[1] * own_weight + spread_total * cache_weight
    numerator = own_part[2] * own_weight[..., None] + spread_sum * cache_weight[..., None]
    live_rows = slot_index[None, :] < prompt_length[:, None]
    attended = jnp.where(
        live_rows[:, None, :, None, None], numerator / denominator[..., None], 0.0
    ).astype(jnp.bfloat16)
    attended = jnp.transpose(attended, (0, 2, 1, 3, 4)).reshape(row_count, -1)
    head_terms = jnp.einsum(
        "sc,ctf->tsf",
        attended,
        output_weight.reshape(output_weight.shape[0], tensor_count, piece_width),
        preferred_element_type=jnp.float32,
    )
    low_part = jnp.einsum(
        "rsc,rkc->rsk",
        attended.reshape(request_number, request_slot_rows, -1),
        output_down_picked,
        preferred_element_type=jnp.float32,
    )
    reduced_output = sum_over_tensor(low_part, tensor_count).astype(jnp.bfloat16)
    head_total = lax.psum_scatter(
        head_terms.astype(jnp.bfloat16), "tensor", scatter_dimension=0, tiled=False
    ).astype(jnp.float32)
    adapter_output = jnp.einsum(
        "ibm,imf->ibf", reduced_output, oup_sel, preferred_element_type=jnp.float32
    ).reshape(row_count, -1)
    return (head_total + ADAPTER_SCALE * adapter_output).astype(jnp.bfloat16)


def solution(mesh):
    placed = (
        P("req", "tensor"),
        P(),
        P(None, "tensor"),
        P(None, "tensor"),
        P("tensor", None),
        P("req", None, "tensor"),
        P("req", None, "tensor"),
        P("req", None, None, "tensor"),
        P("req", None, "tensor"),
        P("req", None, "tensor"),
        P("req"),
        P("req"),
        P(),
        P(),
        P("req", None),
        P("req", None, "tensor"),
    )
    return jax.shard_map(
        local, mesh=mesh, in_specs=placed, out_specs=P("req", "tensor"), check_vma=False
    )
```

```python
import jax
import jax.numpy as jnp
from jax import lax
from jax.sharding import PartitionSpec as P

HEAD_SIZE = 128


ROPE_BASE = 5000000.0
ADAPTER_SCALE = 2.0
EPSILON = 1e-05
NEG_FILL = -1e30


def rotate(vectors, positions):
    half_dim = vectors.shape[-1] // 2
    frequency = ROPE_BASE ** (-jnp.arange(half_dim, dtype=jnp.float32) / half_dim)
    angles = positions.astype(jnp.float32)[..., None] * frequency
    cosine = jnp.cos(angles)
    sine_part = jnp.sin(angles)
    front_half = vectors[..., :half_dim]
    back_half = vectors[..., half_dim:]
    return jnp.concatenate(
        [front_half * cosine - back_half * sine_part, back_half * cosine + front_half * sine_part],
        axis=-1,
    )


def partial_softmax(query_rows, key_rows, value_rows, allowed):
    score_scale = query_rows.shape[-1] ** (-0.5)
    scores = (
        jnp.einsum("bsvgd,bkvd->bvsgk", query_rows, key_rows, preferred_element_type=jnp.float32)
        * score_scale
    )
    spread_mask = allowed[:, None, :, None, :]
    scores = jnp.where(spread_mask, scores, NEG_FILL)
    peak_scores = jnp.max(scores, axis=-1)
    weights = jnp.where(spread_mask, jnp.exp(scores - peak_scores[..., None]), 0.0)
    totals = jnp.sum(weights, axis=-1)
    summed = jnp.einsum(
        "bvsgk,bkvd->bvsgd",
        weights.astype(jnp.bfloat16),
        value_rows,
        preferred_element_type=jnp.float32,
    )
    return (peak_scores, totals, summed)


def gather_by_exchange(piece, axis_name, count):
    spread = jnp.broadcast_to(piece[None], (count,) + piece.shape)
    return lax.all_to_all(spread, axis_name, split_axis=0, concat_axis=0, tiled=True)


def sum_over_tensor(partial, count):
    total = partial.astype(jnp.bfloat16).astype(jnp.float32)
    step = 1
    while step < count:
        pairs = [(index, index ^ step) for index in range(count)]
        sent = total.astype(jnp.bfloat16)
        total = sent.astype(jnp.float32) + lax.ppermute(sent, "tensor", pairs).astype(jnp.float32)
        step *= 2
    return total


def local(
    residual_input,
    input_norm_gain,
    query_weight,
    key_value_weight,
    output_weight,
    adapter_down_maps,
    adapter_query_up,
    adapter_key_value_up,
    adapter_output_down,
    adapter_output_up,
    request_adapter,
    prompt_length,
    cache_length,
    first_page_device,
    page_slot_table,
    cache_page_pool,
):
    holders = lax.axis_size("req")
    tensor_count = lax.axis_size("tensor")
    req_index = lax.axis_index("req")
    tensor_index = lax.axis_index("tensor")
    request_number = request_adapter.shape[0]
    cached_count = request_number // 2
    row_count = residual_input.shape[0]
    request_slot_rows = row_count // request_number
    piece_width = residual_input.shape[1]
    local_kv = key_value_weight.shape[1] // (2 * HEAD_SIZE)
    group_size = query_weight.shape[1] // (HEAD_SIZE * local_kv)
    page_rows = cache_page_pool.shape[1]
    tensor_count = lax.axis_size("tensor")
    chip_count = tensor_count // 2
    core = tensor_index % 2
    chip = tensor_index // 2
    swap = [(index, index ^ 1) for index in range(tensor_count)]
    along = [
        (2 * ((target // 2 - 1) % chip_count), target)
        if target % 2 == 0
        else (2 * ((target // 2 + 1) % chip_count) + 1, target)
        for target in range(tensor_count)
    ]
    partner = lax.ppermute(residual_input, "tensor", swap)
    pair = jnp.where(
        core == 0,
        jnp.concatenate([residual_input, partner], axis=1),
        jnp.concatenate([partner, residual_input], axis=1),
    )
    beside = lax.ppermute(pair, "tensor", along)
    relayed = lax.ppermute(
        lax.dynamic_slice_in_dim(beside, core * piece_width, piece_width, 1), "tensor", along
    )
    held = jnp.concatenate([beside, relayed], axis=1)
    mirrored = lax.ppermute(held, "tensor", swap)
    pair_width = 2 * piece_width
    minus_piece = jnp.where(core == 0, held[:, :pair_width], mirrored[:, :pair_width])
    plus_piece = jnp.where(core == 0, mirrored[:, :pair_width], held[:, :pair_width])
    opposite = jnp.where(
        core == 0,
        jnp.concatenate([held[:, pair_width:], mirrored[:, pair_width:]], axis=1),
        jnp.concatenate([mirrored[:, pair_width:], held[:, pair_width:]], axis=1),
    )
    relative = jnp.stack([pair, plus_piece, opposite, minus_piece])
    chip_order = (jnp.arange(chip_count, dtype=jnp.int32) - chip) % chip_count
    gathered = jnp.take(relative, chip_order, axis=0)
    widened = gathered.astype(jnp.float32)
    inverse = lax.rsqrt(
        jnp.sum(widened * widened, axis=(0, 2), keepdims=True) / (tensor_count * piece_width)
        + EPSILON
    )
    normed_parts = (
        widened * inverse * input_norm_gain.reshape(chip_count, 1, pair_width)
    ).astype(jnp.bfloat16)
    own_normed = (
        residual_input.astype(jnp.float32)
        * inverse[0]
        * lax.dynamic_slice_in_dim(input_norm_gain, tensor_index * piece_width, piece_width, 0)
    ).astype(jnp.bfloat16)
    local_adapters = adapter_down_maps.shape[0]

    def gather_adapters(parts):
        flat_parts = [part.reshape(local_adapters, -1) for part in parts]
        joined = jnp.concatenate(flat_parts, axis=1)
        every = lax.all_gather(
            joined.reshape(local_adapters, joined.shape[1] // 128, 128), "req", axis=0, tiled=True
        )
        return every, flat_parts

    def pick_adapters(parts, every, flat_parts):
        picked = jnp.take(every, request_adapter, axis=0, mode="clip").reshape(
            request_number, -1
        )
        picked_parts = []
        start = 0
        for part, flat in zip(parts, flat_parts):
            width = flat.shape[1]
            picked_parts.append(
                picked[:, start : start + width].reshape((request_number,) + part.shape[1:])
            )
            start += width
        return picked_parts

    up_parts = (adapter_query_up, adapter_key_value_up, adapter_output_down, adapter_output_up)
    every_down, down_flat = gather_adapters((adapter_down_maps,))
    every_down, up_input = lax.optimization_barrier((every_down, up_parts))
    every_up, up_flat = gather_adapters(up_input)
    slot_order = page_slot_table[0].reshape(holders, cached_count).T.reshape(-1)
    outgoing = cache_page_pool[slot_order].reshape(
        cached_count, holders, page_rows, cache_page_pool.shape[2]
    )
    arrived = lax.all_to_all(outgoing, "req", split_axis=1, concat_axis=1, tiled=True)
    every_up, arrived = lax.optimization_barrier((every_up, arrived))
    (down_picked,) = pick_adapters((adapter_down_maps,), every_down, down_flat)
    query_picked, key_value_picked, output_down_picked, oup_sel = pick_adapters(
        up_parts, every_up, up_flat
    )
    adapter_rank_size = query_picked.shape[1]
    own_columns = own_normed.reshape(request_number, request_slot_rows, piece_width)
    partial_low = jnp.einsum(
        "rsd,rkd->rsk", own_columns, down_picked, preferred_element_type=jnp.float32
    )
    reduced_input = sum_over_tensor(partial_low, tensor_count).astype(jnp.bfloat16)
    query_rows = jnp.einsum(
        "csf,cfn->sn",
        normed_parts,
        query_weight.reshape(chip_count, pair_width, -1),
        preferred_element_type=jnp.float32,
    ).reshape(request_number, request_slot_rows, -1)
    query_rows = query_rows + ADAPTER_SCALE * jnp.einsum(
        "ibm,imf->ibf",
        reduced_input[..., :adapter_rank_size],
        query_picked,
        preferred_element_type=jnp.float32,
    )
    keyval = jnp.einsum(
        "csf,cfn->sn",
        normed_parts,
        key_value_weight.reshape(chip_count, pair_width, -1),
        preferred_element_type=jnp.float32,
    ).reshape(
        request_number, request_slot_rows, local_kv, 2 * HEAD_SIZE
    )
    key_add = jnp.einsum(
        "ibm,imf->ibf",
        reduced_input[..., adapter_rank_size : 2 * adapter_rank_size],
        key_value_picked[:, 0],
        preferred_element_type=jnp.float32,
    ).reshape(request_number, request_slot_rows, local_kv, HEAD_SIZE)
    value_add = jnp.einsum(
        "ibm,imf->ibf",
        reduced_input[..., 2 * adapter_rank_size :],
        key_value_picked[:, 1],
        preferred_element_type=jnp.float32,
    ).reshape(request_number, request_slot_rows, local_kv, HEAD_SIZE)
    my_cache = lax.dynamic_slice_in_dim(cache_length, req_index * cached_count, cached_count, 0)
    offsets = jnp.stack([jnp.zeros_like(my_cache), my_cache], axis=1).reshape(request_number)
    slot_index = jnp.arange(request_slot_rows, dtype=jnp.int32)
    positions = offsets[:, None] + slot_index[None, :]
    query_rot = rotate(
        query_rows.reshape(request_number, request_slot_rows, local_kv, group_size, HEAD_SIZE),
        positions[:, :, None, None],
    ).astype(jnp.bfloat16)
    key_rot = rotate(keyval[..., :HEAD_SIZE] + key_add, positions[:, :, None]).astype(jnp.bfloat16)
    value_new = (keyval[..., HEAD_SIZE:] + value_add).astype(jnp.bfloat16)
    causal = slot_index[None, :, None] >= slot_index[None, None, :]
    own_mask = causal & (slot_index[None, None, :] < prompt_length[:, None, None])
    own_part = partial_softmax(query_rot, key_rot, value_new, own_mask)
    asked_queries = query_rot[1::2]
    my_base = lax.dynamic_slice_in_dim(first_page_device, req_index * cached_count, cached_count, 0)
    page_of = (jnp.arange(holders, dtype=jnp.int32)[None, :] - my_base[:, None]) % holders
    key_pos = (
        page_of[:, :, None] * page_rows + jnp.arange(page_rows, dtype=jnp.int32)[None, None, :]
    ).reshape(cached_count, holders * page_rows)
    entries = arrived.reshape(cached_count, holders * page_rows, local_kv, 2 * HEAD_SIZE)
    visible = jnp.broadcast_to(
        (key_pos < my_cache[:, None])[:, None, :],
        (cached_count, request_slot_rows, holders * page_rows),
    )
    cache_part = partial_softmax(
        asked_queries, entries[..., :HEAD_SIZE], entries[..., HEAD_SIZE:], visible
    )
    filler = jnp.full_like(cache_part[0], NEG_FILL)
    spread_peak = jnp.stack([filler, cache_part[0]], axis=1).reshape(own_part[0].shape)
    spread_total = jnp.stack([jnp.zeros_like(cache_part[1]), cache_part[1]], axis=1).reshape(
        own_part[1].shape
    )
    spread_sum = jnp.stack([jnp.zeros_like(cache_part[2]), cache_part[2]], axis=1).reshape(
        own_part[2].shape
    )
    highest_all = jnp.maximum(own_part[0], spread_peak)
    own_weight = jnp.exp(own_part[0] - highest_all)
    cache_weight = jnp.exp(spread_peak - highest_all)
    denominator = own_part[1] * own_weight + spread_total * cache_weight
    numerator = own_part[2] * own_weight[..., None] + spread_sum * cache_weight[..., None]
    live_rows = slot_index[None, :] < prompt_length[:, None]
    attended = jnp.where(
        live_rows[:, None, :, None, None], numerator / denominator[..., None], 0.0
    ).astype(jnp.bfloat16)
    attended = jnp.transpose(attended, (0, 2, 1, 3, 4)).reshape(row_count, -1)
    head_terms = jnp.einsum(
        "sc,ctf->tsf",
        attended,
        output_weight.reshape(output_weight.shape[0], tensor_count, piece_width),
        preferred_element_type=jnp.float32,
    )
    low_part = jnp.einsum(
        "rsc,rkc->rsk",
        attended.reshape(request_number, request_slot_rows, -1),
        output_down_picked,
        preferred_element_type=jnp.float32,
    )
    reduced_output = sum_over_tensor(low_part, tensor_count).astype(jnp.bfloat16)
    head_total = lax.psum_scatter(
        head_terms.astype(jnp.bfloat16), "tensor", scatter_dimension=0, tiled=False
    ).astype(jnp.float32)
    adapter_output = jnp.einsum(
        "ibm,imf->ibf", reduced_output, oup_sel, preferred_element_type=jnp.float32
    ).reshape(row_count, -1)
    return (head_total + ADAPTER_SCALE * adapter_output).astype(jnp.bfloat16)


def solution(mesh):
    placed = (
        P("req", "tensor"),
        P(),
        P(None, "tensor"),
        P(None, "tensor"),
        P("tensor", None),
        P("req", None, "tensor"),
        P("req", None, "tensor"),
        P("req", None, None, "tensor"),
        P("req", None, "tensor"),
        P("req", None, "tensor"),
        P("req"),
        P("req"),
        P(),
        P(),
        P("req", None),
        P("req", None, "tensor"),
    )
    return jax.shard_map(
        local, mesh=mesh, in_specs=placed, out_specs=P("req", "tensor"), check_vma=False
    )
```
